128 devices in a mesh: space: 32 (over y, x, core), shell: 4 (over z).
Axes of the slice: x: 4, y: 4, z: 4, core: 2. Of those that a mesh axis runs over, the one named last changes fastest.
Arguments:
- weights: float32 [262144], P(('space', 'shell')), may hold values from 0.02 to 1.5
- seg_streamline: int32 [32, 4, 32, 256], P('space', 'shell'), may hold values from 0 to 2047
- seg_features: float32 [32, 4, 32, 256, 128], P('space', 'shell'), may hold values from -12 to 12
- pair_counts: int32 [32, 4, 32], P('space', 'shell'), may hold values from 32 to 256, as said below
- seg_voxel: int32 [32, 4, 32, 256], P('space', 'shell'), may hold values from 0 to 4095
- dictionary: float32 [128, 256], P(None, 'shell'), may hold values from -0.375 to 0.375
- measured: float32 [256, 131072], P('shell', 'space'), may hold values from -6 to 6
Outputs:
- new_weights: float32 [262144], P(('space', 'shell'))
- residual: float32 [256, 131072], P('shell', 'space')
The draws below stay inside these ranges and needn't reach their ends.
Inputs may be any that keep to these rules, and one draw needn't show every extreme that they name: In each shell group q one voxel block d has pair_counts[s, q, d] = 256 for every s.
All inputs are finite; a program needn't handle non-finite values.
Results may differ from the reference program's by a relative error of at most 0.0003.
Values sent between devices are 32-bit elements; how exact they have to be, the bound alone decides.
No kernel may reach another device: no remote copies, remote signals or barrier semaphores. Data moves between devices by JAX's collectives and lax.ppermute only.
A program may use at most 64 MiB of HBM per device.

```python
import math
import jax
import jax.numpy as jnp
from jax import lax

DIRS = 256
COEFFS = 128
VOX_DEV = 4096
STR_DEV = 2048
CAP = 256
ITERS = 2
VBLOCKS = 32
SHELLS = 4
VOXELS = 131072
STREAMLINES = 262144


def draw_seg_features(key, part):
    key_base = jax.random.fold_in(key, 11)
    key_len = jax.random.fold_in(key, 12)
    key_col = jax.random.fold_in(key, 13)
    full_shape = (VBLOCKS, SHELLS, VBLOCKS, CAP, COEFFS)
    base_draw = jnp.clip(jax.random.normal(key_base, full_shape, jnp.float32), -4.0, 4.0)
    seglen = jnp.exp(jax.random.uniform(key_len, (VBLOCKS, SHELLS, VBLOCKS, CAP, 1), jnp.float32, math.log(0.1), math.log(2.0)))
    column = jnp.exp(jax.random.uniform(key_col, (COEFFS,), jnp.float32, math.log(0.3), math.log(3.0)))
    return 0.5 * base_draw * seglen * column


def draw_pair_counts(key, part):
    key_base = jax.random.fold_in(key, 21)
    key_hot = jax.random.fold_in(key, 22)
    base_draw = jax.random.randint(key_base, (VBLOCKS, SHELLS, VBLOCKS), max(1, CAP // 8), CAP // 2 + 1, jnp.int32)
    hot_block = jax.random.randint(key_hot, (SHELLS,), 0, VBLOCKS, jnp.int32)
    target = jnp.arange(VBLOCKS, dtype=jnp.int32)[None, None, :]
    return jnp.where(target == hot_block[None, :, None], jnp.int32(CAP), base_draw)


def touch_ends(result, stream_key, least, high):
    place = [jax.random.randint(jax.random.fold_in(stream_key, axis), (), 0, length) for axis, length in enumerate(result.shape)]
    main_axis = result.shape.index(max(result.shape))
    beside = place[:main_axis] + [(place[main_axis] + 1) % result.shape[main_axis]] + place[main_axis + 1:]
    return result.at[tuple(place)].set(least).at[tuple(beside)].set(high)


def shard_levels(own_key, shape, split, low, top_value):
    factor_of = 1.0
    for axis_at, shards_of in split:
        draws = jax.random.uniform(jax.random.fold_in(jax.random.fold_in(own_key, 6), axis_at), (shards_of,), jnp.float32, low / len(split), top_value / len(split))
        factor_of = factor_of * jnp.repeat(jnp.exp(draws), shape[axis_at] // shards_of).reshape((-1,) + (1,) * (len(shape) - 1 - axis_at))
    return factor_of


def scatter_about(rng, dims, scale, most, split=(), kind=jnp.bfloat16):
    result = jax.random.normal(rng, dims, jnp.float32) * scale
    if len(split) > 0:
        result = shard_levels(rng, dims, split, -0.22, 0.18) * result
    return jnp.clip(result, min=-most, max=most).astype(kind)


def setup_inputs(seed: int = 0) -> dict:
    streams_of = jax.random.split(jax.random.key(seed), 8)
    weights = jnp.clip(0.02 + 1.48 * jax.random.uniform(streams_of[0], (STREAMLINES,), jnp.float32) ** shard_levels(streams_of[0], (STREAMLINES,), ((0, 128),), -0.2, 0.2), 0.02, 1.5)
    seg_streamline = touch_ends(jax.random.randint(streams_of[1], (VBLOCKS, SHELLS, VBLOCKS, CAP), 0, STR_DEV), jax.random.fold_in(streams_of[1], 1), 0, STR_DEV - 1).astype(jnp.int32)
    seg_features = draw_seg_features(jax.random.fold_in(streams_of[7], 71), 0)
    pair_counts = draw_pair_counts(jax.random.fold_in(streams_of[7], 71), 0)
    seg_voxel = touch_ends(jax.random.randint(streams_of[4], (VBLOCKS, SHELLS, VBLOCKS, CAP), 0, VOX_DEV), jax.random.fold_in(streams_of[4], 1), 0, VOX_DEV - 1).astype(jnp.int32)
    dictionary = scatter_about(streams_of[5], (COEFFS, DIRS), DIRS ** -0.5, 0.375, ((1, 4),), jnp.float32)
    measured = scatter_about(streams_of[6], (DIRS, VOXELS), 1.0, 6.0, ((0, 4), (1, 32)), jnp.float32)
    return dict(weights=weights, seg_streamline=seg_streamline, seg_features=seg_features, pair_counts=pair_counts, seg_voxel=seg_voxel, dictionary=dictionary, measured=measured)


def reference(weights, seg_streamline, seg_features, pair_counts, seg_voxel, dictionary, measured):
    slot_pos = jnp.arange(CAP, dtype=jnp.int32)[None, None, None, :]
    live_slot = slot_pos < pair_counts[..., None]
    features = jnp.where(live_slot[..., None], seg_features, jnp.float32(0.0))
    source = jnp.arange(VBLOCKS, dtype=jnp.int32)[:, None, None, None]
    shell_pos = jnp.arange(SHELLS, dtype=jnp.int32)[None, :, None, None]
    target = jnp.arange(VBLOCKS, dtype=jnp.int32)[None, None, :, None]
    owner_index = ((source * SHELLS + shell_pos) * STR_DEV + seg_streamline).astype(jnp.int32)
    voxel_flat = (target * VOX_DEV + jnp.transpose(seg_voxel, (2, 1, 0, 3))).astype(jnp.int32)
    column_sq = jnp.zeros((STREAMLINES,), jnp.float32).at[owner_index].add(jnp.sum(features * features, axis=-1))
    scaling = 0.5 / (0.5 + column_sq)
    current = weights
    residual = jnp.zeros((DIRS, VOXELS), jnp.float32)
    for iteration in range(ITERS):
        seg_terms = current[owner_index][..., None] * features
        coeff = jnp.zeros((VOXELS, COEFFS), jnp.float32).at[voxel_flat].add(seg_terms)
        residual = jnp.einsum("jg,vj->gv", dictionary, coeff, precision=lax.Precision.HIGHEST) - measured
        adjoint = jnp.einsum("gv,jg->vj", residual, dictionary, precision=lax.Precision.HIGHEST)
        grad_slot = jnp.sum(features * adjoint[voxel_flat], axis=-1)
        gradient = jnp.zeros((STREAMLINES,), jnp.float32).at[owner_index].add(grad_slot)
        current = jnp.maximum(current - scaling * gradient, 0.0)
    return current, residual
```

```python
import jax
import jax.numpy as jnp
from jax import lax
from jax.sharding import PartitionSpec as P

ITERS = 2
HI = lax.Precision.HIGHEST


def one_hot_pair(index, count):
    low_count = 64
    high_count = count // low_count
    flat = index.reshape(-1)
    high = (flat // low_count)[:, None] == lax.broadcasted_iota(jnp.int32, (1, high_count), 1)
    low = (flat % low_count)[:, None] == lax.broadcasted_iota(jnp.int32, (1, low_count), 1)
    return high.astype(jnp.float32), low.astype(jnp.float32)


def pick(table, high, low):
    rows = jnp.dot(high, table.reshape(high.shape[1], low.shape[1]), precision=HI)
    return jnp.sum(rows * low, axis=1)


def spread(values, high, low):
    return jnp.dot(high.T, values.reshape(-1)[:, None] * low, precision=HI).reshape(-1)


def on_device(weights, seg_streamline, seg_features, pair_counts, seg_voxel, dictionary, measured):
    blocks = seg_streamline.shape[2]
    slots = seg_streamline.shape[3]
    coeffs = seg_features.shape[4]
    streams = weights.shape[0]
    stream_index = seg_streamline.reshape(blocks, slots)
    voxel_index = seg_voxel.reshape(blocks * slots)
    counts = pair_counts.reshape(blocks)
    live_slot = lax.broadcasted_iota(jnp.int32, (blocks, slots), 1) < counts[:, None]
    masked = jnp.where(
        live_slot[:, :, None], seg_features.reshape(blocks, slots, coeffs), jnp.float32(0.0)
    )
    local_feat = lax.all_to_all(masked, "space", split_axis=0, concat_axis=0, tiled=True)
    local_feat = local_feat.reshape(blocks * slots, coeffs)
    gram = lax.psum(jnp.dot(dictionary, dictionary.T, precision=HI), "shell")
    data_proj = lax.psum(jnp.dot(measured.T, dictionary.T, precision=HI), "shell")
    high, low = one_hot_pair(stream_index, streams)
    column_sq = spread(jnp.sum(masked * masked, axis=2), high, low)
    scaling = 0.5 / (0.5 + column_sq)
    current = weights
    residual = jnp.zeros(measured.shape, jnp.float32)
    for iteration in range(ITERS):
        picked = pick(current, high, low).reshape(blocks, slots)
        local_x = lax.all_to_all(picked, "space", split_axis=0, concat_axis=0, tiled=True)
        seg_terms = local_x.reshape(blocks * slots, 1) * local_feat
        partial_coeff = (
            jnp.zeros((measured.shape[1], coeffs), jnp.float32).at[voxel_index].add(seg_terms)
        )
        coeff_sum = lax.psum(partial_coeff, "shell")
        if iteration == ITERS - 1:
            residual = (
                jnp.einsum("jg,vj->gv", dictionary, coeff_sum, precision=HI) - measured
            )
        adjoint = jnp.dot(coeff_sum, gram, precision=HI) - data_proj
        local_grad = jnp.sum(local_feat * adjoint[voxel_index], axis=1).reshape(blocks, slots)
        grad_slot = lax.all_to_all(local_grad, "space", split_axis=0, concat_axis=0, tiled=True)
        gradient = spread(grad_slot, high, low)
        current = jnp.maximum(current - scaling * gradient, 0.0)
    return (current, residual)


def solution(mesh):
    in_specs = (
        P(("space", "shell")),
        P("space", "shell", None, None),
        P("space", "shell", None, None, None),
        P("space", "shell", None),
        P("space", "shell", None, None),
        P(None, "shell"),
        P("shell", "space"),
    )
    out_specs = (P(("space", "shell")), P("shell", "space"))
    return jax.shard_map(
        on_device, mesh=mesh, in_specs=in_specs, out_specs=out_specs, check_vma=False
    )
```

```python
import jax
import jax.numpy as jnp
from jax import lax
from jax.sharding import PartitionSpec as P

ITERS = 2
HI = lax.Precision.HIGHEST


def one_hot_pair(index, count):
    low_count = 64
    high_count = count // low_count
    flat = index.reshape(-1)
    high = (flat // low_count)[:, None] == lax.broadcasted_iota(jnp.int32, (1, high_count), 1)
    low = (flat % low_count)[:, None] == lax.broadcasted_iota(jnp.int32, (1, low_count), 1)
    return high.astype(jnp.float32), low.astype(jnp.float32)


def pick(table, high, low):
    rows = jnp.dot(high, table.reshape(high.shape[1], low.shape[1]), precision=HI)
    return jnp.sum(rows * low, axis=1)


def spread(values, high, low):
    return jnp.dot(high.T, values.reshape(-1)[:, None] * low, precision=HI).reshape(-1)


def on_device(weights, seg_streamline, seg_features, pair_counts, seg_voxel, dictionary, measured):
    blocks = seg_streamline.shape[2]
    slots = seg_streamline.shape[3]
    coeffs = seg_features.shape[4]
    streams = weights.shape[0]
    stream_index = seg_streamline.reshape(blocks, slots)
    voxel_index = seg_voxel.reshape(blocks * slots)
    counts = pair_counts.reshape(blocks)
    live_slot = lax.broadcasted_iota(jnp.int32, (blocks, slots), 1) < counts[:, None]
    masked = jnp.where(
        live_slot[:, :, None], seg_features.reshape(blocks, slots, coeffs), jnp.float32(0.0)
    )
    half = slots // 2
    feat_parts = [
        lax.all_to_all(masked[:, h * half:(h + 1) * half], "space", 0, 0, tiled=True)
        for h in range(2)
    ]
    gram = lax.psum(jnp.dot(dictionary, dictionary.T, precision=HI), "shell")
    data_proj = lax.psum(jnp.dot(measured.T, dictionary.T, precision=HI), "shell")
    feat_parts[1], gram, data_proj = lax.optimization_barrier((feat_parts[1], gram, data_proj))
    vox_parts = [voxel_index.reshape(blocks, slots)[:, h * half:(h + 1) * half].reshape(-1)
                 for h in range(2)]
    local_feat = jnp.concatenate(feat_parts, axis=1).reshape(blocks * slots, coeffs)
    high, low = one_hot_pair(stream_index, streams)
    column_sq = spread(jnp.sum(masked * masked, axis=2), high, low)
    scaling = 0.5 / (0.5 + column_sq)
    current = weights
    residual = jnp.zeros(measured.shape, jnp.float32)
    for iteration in range(ITERS):
        picked = pick(current, high, low).reshape(blocks, slots)
        local_x = lax.all_to_all(picked, "space", split_axis=0, concat_axis=0, tiled=True)
        partial_coeff = jnp.zeros((measured.shape[1], coeffs), jnp.float32)
        for h in range(2):
            part_x = local_x[:, h * half:(h + 1) * half].reshape(-1, 1)
            partial_coeff = partial_coeff.at[vox_parts[h]].add(
                part_x * feat_parts[h].reshape(-1, coeffs)
            )
        coeff_sum = lax.psum(partial_coeff, "shell")
        if iteration == ITERS - 1:
            residual = (
                jnp.einsum("jg,vj->gv", dictionary, coeff_sum, precision=HI) - measured
            )
        adjoint = jnp.dot(coeff_sum, gram, precision=HI) - data_proj
        local_grad = jnp.sum(local_feat * adjoint[voxel_index], axis=1).reshape(blocks, slots)
        grad_slot = lax.all_to_all(local_grad, "space", split_axis=0, concat_axis=0, tiled=True)
        gradient = spread(grad_slot, high, low)
        current = jnp.maximum(current - scaling * gradient, 0.0)
    return (current, residual)


def solution(mesh):
    in_specs = (
        P(("space", "shell")),
        P("space", "shell", None, None),
        P("space", "shell", None, None, None),
        P("space", "shell", None),
        P("space", "shell", None, None),
        P(None, "shell"),
        P("shell", "space"),
    )
    out_specs = (P(("space", "shell")), P("shell", "space"))
    return jax.shard_map(
        on_device, mesh=mesh, in_specs=in_specs, out_specs=out_specs, check_vma=False
    )
```

```python
import jax
import jax.numpy as jnp
from jax import lax
from jax.sharding import PartitionSpec as P
from jax.experimental import pallas as pl
from jax.experimental.pallas import tpu as pltpu

ITERS = 2
HI = lax.Precision.HIGHEST


def one_hot_pair(index, count):
    low_count = 64
    high_count = count // low_count
    flat = index.reshape(-1)
    high = (flat // low_count)[:, None] == lax.broadcasted_iota(jnp.int32, (1, high_count), 1)
    low = (flat % low_count)[:, None] == lax.broadcasted_iota(jnp.int32, (1, low_count), 1)
    return high.astype(jnp.float32), low.astype(jnp.float32)


def pick(table, high, low):
    rows = jnp.dot(high, table.reshape(high.shape[1], low.shape[1]), precision=HI)
    return jnp.sum(rows * low, axis=1)


def spread(values, high, low):
    return jnp.dot(high.T, values.reshape(-1)[:, None] * low, precision=HI).reshape(-1)


UNROLL = 8
ACCS = 4


def scatter_kernel(idx_ref, xs_ref, feat_ref, init_ref, out_ref, *accs):
    accs[0][...] = init_ref[...]
    for acc in accs[1:]:
        acc[...] = jnp.zeros(acc.shape, acc.dtype)

    def body(step, carry):
        for u in range(UNROLL):
            k = step * UNROLL + u
            acc = accs[u % ACCS]
            acc[pl.ds(idx_ref[k], 1), :] += xs_ref[k] * feat_ref[pl.ds(k, 1), :]
        return carry

    lax.fori_loop(0, feat_ref.shape[0] // UNROLL, body, 0)
    total = accs[0][...]
    for acc in accs[1:]:
        total = total + acc[...]
    out_ref[...] = total


def row_scatter(idx, xs, feat, init):
    smem = pl.BlockSpec(memory_space=pltpu.SMEM)
    vmem = pl.BlockSpec(memory_space=pltpu.VMEM)
    return pl.pallas_call(
        scatter_kernel,
        out_shape=jax.ShapeDtypeStruct(init.shape, jnp.float32),
        in_specs=[smem, smem, vmem, vmem],
        out_specs=vmem,
        scratch_shapes=[pltpu.VMEM(init.shape, jnp.float32) for _ in range(ACCS)],
    )(idx, xs, feat, init)


def gather_kernel(idx_ref, table_ref, feat_ref, out_ref, rows_ref):
    def body(step, carry):
        for u in range(UNROLL):
            k = step * UNROLL + u
            rows_ref[pl.ds(k, 1), :] = table_ref[pl.ds(idx_ref[k], 1), :]
        return carry

    lax.fori_loop(0, feat_ref.shape[0] // UNROLL, body, 0)
    out_ref[...] = jnp.sum(rows_ref[...] * feat_ref[...], axis=1, keepdims=True)


def row_gather_dot(idx, table, feat):
    smem = pl.BlockSpec(memory_space=pltpu.SMEM)
    vmem = pl.BlockSpec(memory_space=pltpu.VMEM)
    return pl.pallas_call(
        gather_kernel,
        out_shape=jax.ShapeDtypeStruct((feat.shape[0], 1), jnp.float32),
        in_specs=[smem, vmem, vmem],
        out_specs=vmem,
        scratch_shapes=[pltpu.VMEM(feat.shape, jnp.float32)],
    )(idx, table, feat)


def on_device(weights, seg_streamline, seg_features, pair_counts, seg_voxel, dictionary, measured):
    blocks = seg_streamline.shape[2]
    slots = seg_streamline.shape[3]
    coeffs = seg_features.shape[4]
    streams = weights.shape[0]
    stream_index = seg_streamline.reshape(blocks, slots)
    voxel_index = seg_voxel.reshape(blocks * slots)
    counts = pair_counts.reshape(blocks)
    live_slot = lax.broadcasted_iota(jnp.int32, (blocks, slots), 1) < counts[:, None]
    masked = jnp.where(
        live_slot[:, :, None], seg_features.reshape(blocks, slots, coeffs), jnp.float32(0.0)
    )
    half = slots // 2
    feat_parts = [
        lax.all_to_all(masked[:, h * half:(h + 1) * half], "space", 0, 0, tiled=True)
        for h in range(2)
    ]
    gram = lax.psum(jnp.dot(dictionary, dictionary.T, precision=HI), "shell")
    data_proj = lax.psum(jnp.dot(measured.T, dictionary.T, precision=HI), "shell")
    feat_parts[1], gram, data_proj = lax.optimization_barrier((feat_parts[1], gram, data_proj))
    vox_parts = [voxel_index.reshape(blocks, slots)[:, h * half:(h + 1) * half].reshape(-1)
                 for h in range(2)]
    local_feat = jnp.concatenate(feat_parts, axis=1).reshape(blocks * slots, coeffs)
    high, low = one_hot_pair(stream_index, streams)
    column_sq = spread(jnp.sum(masked * masked, axis=2), high, low)
    scaling = 0.5 / (0.5 + column_sq)
    current = weights
    residual = jnp.zeros(measured.shape, jnp.float32)
    for iteration in range(ITERS):
        picked = pick(current, high, low).reshape(blocks, slots)
        local_x = lax.all_to_all(picked, "space", split_axis=0, concat_axis=0, tiled=True)
        partial_coeff = jnp.zeros((measured.shape[1], coeffs), jnp.float32)
        for h in range(2):
            part_x = local_x[:, h * half:(h + 1) * half].reshape(-1)
            partial_coeff = row_scatter(
                vox_parts[h], part_x, feat_parts[h].reshape(-1, coeffs), partial_coeff
            )
        coeff_sum = lax.psum(partial_coeff, "shell")
        if iteration == ITERS - 1:
            residual = (
                jnp.einsum("jg,vj->gv", dictionary, coeff_sum, precision=HI) - measured
            )
        adjoint = jnp.dot(coeff_sum, gram, precision=HI) - data_proj
        local_grad = row_gather_dot(voxel_index, adjoint, local_feat).reshape(blocks, slots)
        grad_slot = lax.all_to_all(local_grad, "space", split_axis=0, concat_axis=0, tiled=True)
        gradient = spread(grad_slot, high, low)
        current = jnp.maximum(current - scaling * gradient, 0.0)
    return (current, residual)


def solution(mesh):
    in_specs = (
        P(("space", "shell")),
        P("space", "shell", None, None),
        P("space", "shell", None, None, None),
        P("space", "shell", None),
        P("space", "shell", None, None),
        P(None, "shell"),
        P("shell", "space"),
    )
    out_specs = (P(("space", "shell")), P("shell", "space"))
    return jax.shard_map(
        on_device, mesh=mesh, in_specs=in_specs, out_specs=out_specs, check_vma=False
    )
```

```python
import jax
import jax.numpy as jnp
from jax import lax
from jax.sharding import PartitionSpec as P
from jax.experimental import pallas as pl
from jax.experimental.pallas import tpu as pltpu

ITERS = 2
HI = lax.Precision.HIGHEST


def one_hot_pair(index, count):
    low_count = 64
    high_count = count // low_count
    flat = index.reshape(-1)
    high = (flat // low_count)[:, None] == lax.broadcasted_iota(jnp.int32, (1, high_count), 1)
    low = (flat % low_count)[:, None] == lax.broadcasted_iota(jnp.int32, (1, low_count), 1)
    return high.astype(jnp.float32), low.astype(jnp.float32)


def pick(table, high, low):
    rows = jnp.dot(high, table.reshape(high.shape[1], low.shape[1]), precision=HI)
    return jnp.sum(rows * low, axis=1)


def spread(values, high, low):
    return jnp.dot(high.T, values.reshape(-1)[:, None] * low, precision=HI).reshape(-1)


UNROLL = 8
ACCS = 4


def scatter_kernel(idx_ref, xs_ref, feat_ref, init_ref, out_ref, *accs):
    accs[0][...] = init_ref[...]
    for acc in accs[1:]:
        acc[...] = jnp.zeros(acc.shape, acc.dtype)

    def body(step, carry):
        for u in range(UNROLL):
            k = step * UNROLL + u
            acc = accs[u % ACCS]
            acc[pl.ds(idx_ref[k], 1), :] += xs_ref[k] * feat_ref[pl.ds(k, 1), :]
        return carry

    lax.fori_loop(0, feat_ref.shape[0] // UNROLL, body, 0)
    total = accs[0][...]
    for acc in accs[1:]:
        total = total + acc[...]
    out_ref[...] = total


def row_scatter(idx, xs, feat, init):
    smem = pl.BlockSpec(memory_space=pltpu.SMEM)
    vmem = pl.BlockSpec(memory_space=pltpu.VMEM)
    return pl.pallas_call(
        scatter_kernel,
        out_shape=jax.ShapeDtypeStruct(init.shape, jnp.float32),
        in_specs=[smem, smem, vmem, vmem],
        out_specs=vmem,
        scratch_shapes=[pltpu.VMEM(init.shape, jnp.float32) for _ in range(ACCS)],
    )(idx, xs, feat, init)


def gather_kernel(idx_ref, table_ref, feat_ref, out_ref, rows_ref):
    def body(step, carry):
        for u in range(UNROLL):
            k = step * UNROLL + u
            rows_ref[pl.ds(k, 1), :] = table_ref[pl.ds(idx_ref[k], 1), :]
        return carry

    lax.fori_loop(0, feat_ref.shape[0] // UNROLL, body, 0)
    out_ref[...] = jnp.sum(rows_ref[...] * feat_ref[...], axis=1, keepdims=True)


def row_gather_dot(idx, table, feat):
    smem = pl.BlockSpec(memory_space=pltpu.SMEM)
    vmem = pl.BlockSpec(memory_space=pltpu.VMEM)
    return pl.pallas_call(
        gather_kernel,
        out_shape=jax.ShapeDtypeStruct((feat.shape[0], 1), jnp.float32),
        in_specs=[smem, vmem, vmem],
        out_specs=vmem,
        scratch_shapes=[pltpu.VMEM(feat.shape, jnp.float32)],
    )(idx, table, feat)


def on_device(weights, seg_streamline, seg_features, pair_counts, seg_voxel, dictionary, measured):
    blocks = seg_streamline.shape[2]
    slots = seg_streamline.shape[3]
    coeffs = seg_features.shape[4]
    streams = weights.shape[0]
    stream_index = seg_streamline.reshape(blocks, slots)
    voxel_index = seg_voxel.reshape(blocks * slots)
    counts = pair_counts.reshape(blocks)
    live_slot = lax.broadcasted_iota(jnp.int32, (blocks, slots), 1) < counts[:, None]
    masked = jnp.where(
        live_slot[:, :, None], seg_features.reshape(blocks, slots, coeffs), jnp.float32(0.0)
    )
    high, low = one_hot_pair(stream_index, streams)
    column_sq = spread(jnp.sum(masked * masked, axis=2), high, low)
    scaling = 0.5 / (0.5 + column_sq)
    half = slots // 2
    picked = pick(weights, high, low).reshape(blocks, slots // coeffs, coeffs)
    pad_rows = 8 - slots // coeffs
    first = jnp.concatenate(
        [masked[:, :half], picked, jnp.zeros((blocks, pad_rows, coeffs), jnp.float32)], axis=1
    )
    first = lax.all_to_all(first, "space", 0, 0, tiled=True)
    feat_parts = [
        first[:, :half],
        lax.all_to_all(masked[:, half:], "space", 0, 0, tiled=True),
    ]
    local_x = first[:, half:half + slots // coeffs].reshape(blocks, slots)
    gram = lax.psum(jnp.dot(dictionary, dictionary.T, precision=HI), "shell")
    shell_proj = jnp.dot(measured.T, dictionary.T, precision=HI)
    vox_parts = [voxel_index.reshape(blocks, slots)[:, h * half:(h + 1) * half].reshape(-1)
                 for h in range(2)]
    local_feat = jnp.concatenate(feat_parts, axis=1).reshape(blocks * slots, coeffs)
    current = weights
    residual = jnp.zeros(measured.shape, jnp.float32)
    data_proj = None
    for iteration in range(ITERS):
        if iteration > 0:
            picked = pick(current, high, low).reshape(blocks, slots)
            local_x = lax.all_to_all(picked, "space", split_axis=0, concat_axis=0, tiled=True)
            if data_proj is not None:
                data_proj, local_x = lax.optimization_barrier((data_proj, local_x))
        partial_coeff = jnp.zeros((measured.shape[1], coeffs), jnp.float32)
        for h in range(2):
            part_x = local_x[:, h * half:(h + 1) * half].reshape(-1)
            partial_coeff = row_scatter(
                vox_parts[h], part_x, feat_parts[h].reshape(-1, coeffs), partial_coeff
            )
        if iteration < ITERS - 1:
            adjoint = lax.psum(jnp.dot(partial_coeff, gram, precision=HI) - shell_proj, "shell")
            if data_proj is None:
                shell_proj, adjoint = lax.optimization_barrier((shell_proj, adjoint))
                data_proj = lax.psum(shell_proj, "shell")
        else:
            coeff_sum = lax.psum(partial_coeff, "shell")
            residual = (
                jnp.einsum("jg,vj->gv", dictionary, coeff_sum, precision=HI) - measured
            )
            if data_proj is None:
                data_proj = lax.psum(shell_proj, "shell")
            adjoint = jnp.dot(coeff_sum, gram, precision=HI) - data_proj
        local_grad = row_gather_dot(voxel_index, adjoint, local_feat).reshape(blocks, slots)
        grad_slot = lax.all_to_all(local_grad, "space", split_axis=0, concat_axis=0, tiled=True)
        gradient = spread(grad_slot, high, low)
        current = jnp.maximum(current - scaling * gradient, 0.0)
    return (current, residual)


def solution(mesh):
    in_specs = (
        P(("space", "shell")),
        P("space", "shell", None, None),
        P("space", "shell", None, None, None),
        P("space", "shell", None),
        P("space", "shell", None, None),
        P(None, "shell"),
        P("shell", "space"),
    )
    out_specs = (P(("space", "shell")), P("shell", "space"))
    return jax.shard_map(
        on_device, mesh=mesh, in_specs=in_specs, out_specs=out_specs, check_vma=False
    )
```

```python
import jax
import jax.numpy as jnp
from jax import lax
from jax.sharding import PartitionSpec as P
from jax.experimental import pallas as pl
from jax.experimental.pallas import tpu as pltpu

ITERS = 2
HI = lax.Precision.HIGHEST


def one_hot_pair(index, count):
    low_count = 64
    high_count = count // low_count
    flat = index.reshape(-1)
    high = (flat // low_count)[:, None] == lax.broadcasted_iota(jnp.int32, (1, high_count), 1)
    low = (flat % low_count)[:, None] == lax.broadcasted_iota(jnp.int32, (1, low_count), 1)
    return high.astype(jnp.float32), low.astype(jnp.float32)


def pick(table, high, low):
    rows = jnp.dot(high, table.reshape(high.shape[1], low.shape[1]), precision=HI)
    return jnp.sum(rows * low, axis=1)


def spread(values, high, low):
    return jnp.dot(high.T, values.reshape(-1)[:, None] * low, precision=HI).reshape(-1)


UNROLL = 8
ACCS = 4


def scatter_kernel(idx_ref, xs_ref, feat_ref, init_ref, out_ref, *accs):
    accs[0][...] = init_ref[...]
    for acc in accs[1:]:
        acc[...] = jnp.zeros(acc.shape, acc.dtype)

    def body(step, carry):
        for u in range(UNROLL):
            k = step * UNROLL + u
            acc = accs[u % ACCS]
            acc[pl.ds(idx_ref[k], 1), :] += xs_ref[k] * feat_ref[pl.ds(k, 1), :]
        return carry

    lax.fori_loop(0, feat_ref.shape[0] // UNROLL, body, 0)
    total = accs[0][...]
    for acc in accs[1:]:
        total = total + acc[...]
    out_ref[...] = total


def row_scatter(idx, xs, feat, init):
    smem = pl.BlockSpec(memory_space=pltpu.SMEM)
    vmem = pl.BlockSpec(memory_space=pltpu.VMEM)
    return pl.pallas_call(
        scatter_kernel,
        out_shape=jax.ShapeDtypeStruct(init.shape, jnp.float32),
        in_specs=[smem, smem, vmem, vmem],
        out_specs=vmem,
        scratch_shapes=[pltpu.VMEM(init.shape, jnp.float32) for _ in range(ACCS)],
    )(idx, xs, feat, init)


def gather_kernel(idx_ref, table_ref, feat_ref, out_ref, rows_ref):
    def body(step, carry):
        for u in range(UNROLL):
            k = step * UNROLL + u
            rows_ref[pl.ds(k, 1), :] = table_ref[pl.ds(idx_ref[k], 1), :]
        return carry

    lax.fori_loop(0, feat_ref.shape[0] // UNROLL, body, 0)
    lanes = out_ref.shape[1]

    def reduce_block(block, carry):
        start = pl.multiple_of(block * lanes, lanes)
        prod = rows_ref[pl.ds(start, lanes), :] * feat_ref[pl.ds(start, lanes), :]
        out_ref[pl.ds(block, 1), :] = jnp.sum(prod.T, axis=0, keepdims=True)
        return carry

    lax.fori_loop(0, out_ref.shape[0], reduce_block, 0)


def row_gather_dot(idx, table, feat):
    smem = pl.BlockSpec(memory_space=pltpu.SMEM)
    vmem = pl.BlockSpec(memory_space=pltpu.VMEM)
    return pl.pallas_call(
        gather_kernel,
        out_shape=jax.ShapeDtypeStruct((feat.shape[0] // 128, 128), jnp.float32),
        in_specs=[smem, vmem, vmem],
        out_specs=vmem,
        scratch_shapes=[pltpu.VMEM(feat.shape, jnp.float32)],
    )(idx, table, feat)


def on_device(weights, seg_streamline, seg_features, pair_counts, seg_voxel, dictionary, measured):
    blocks = seg_streamline.shape[2]
    slots = seg_streamline.shape[3]
    coeffs = seg_features.shape[4]
    streams = weights.shape[0]
    stream_index = seg_streamline.reshape(blocks, slots)
    voxel_index = seg_voxel.reshape(blocks * slots)
    counts = pair_counts.reshape(blocks)
    live_slot = lax.broadcasted_iota(jnp.int32, (blocks, slots), 1) < counts[:, None]
    masked = jnp.where(
        live_slot[:, :, None], seg_features.reshape(blocks, slots, coeffs), jnp.float32(0.0)
    )
    half = slots // 2
    feat_parts = [
        lax.all_to_all(masked[:, h * half:(h + 1) * half], "space", 0, 0, tiled=True)
        for h in range(2)
    ]
    gram = lax.psum(jnp.dot(dictionary, dictionary.T, precision=HI), "shell")
    data_proj = lax.psum(jnp.dot(measured.T, dictionary.T, precision=HI), "shell")
    feat_parts[1], gram, data_proj = lax.optimization_barrier((feat_parts[1], gram, data_proj))
    vox_parts = [voxel_index.reshape(blocks, slots)[:, h * half:(h + 1) * half].reshape(-1)
                 for h in range(2)]
    local_feat = jnp.concatenate(feat_parts, axis=1).reshape(blocks * slots, coeffs)
    high, low = one_hot_pair(stream_index, streams)
    column_sq = spread(jnp.sum(masked * masked, axis=2), high, low)
    scaling = 0.5 / (0.5 + column_sq)
    current = weights
    residual = jnp.zeros(measured.shape, jnp.float32)
    for iteration in range(ITERS):
        picked = pick(current, high, low).reshape(blocks, slots)
        local_x = lax.all_to_all(picked, "space", split_axis=0, concat_axis=0, tiled=True)
        partial_coeff = jnp.zeros((measured.shape[1], coeffs), jnp.float32)
        if iteration == 0:
            for h in range(2):
                part_x = local_x[:, h * half:(h + 1) * half].reshape(-1)
                partial_coeff = row_scatter(
                    vox_parts[h], part_x, feat_parts[h].reshape(-1, coeffs), partial_coeff
                )
        else:
            partial_coeff = row_scatter(
                voxel_index, local_x.reshape(-1), local_feat, partial_coeff
            )
        coeff_sum = lax.psum(partial_coeff, "shell")
        if iteration == ITERS - 1:
            residual = (
                jnp.einsum("jg,vj->gv", dictionary, coeff_sum, precision=HI) - measured
            )
        adjoint = jnp.dot(coeff_sum, gram, precision=HI) - data_proj
        local_grad = row_gather_dot(voxel_index, adjoint, local_feat).reshape(blocks, slots)
        grad_slot = lax.all_to_all(local_grad, "space", split_axis=0, concat_axis=0, tiled=True)
        gradient = spread(grad_slot, high, low)
        current = jnp.maximum(current - scaling * gradient, 0.0)
    return (current, residual)


def solution(mesh):
    in_specs = (
        P(("space", "shell")),
        P("space", "shell", None, None),
        P("space", "shell", None, None, None),
        P("space", "shell", None),
        P("space", "shell", None, None),
        P(None, "shell"),
        P("shell", "space"),
    )
    out_specs = (P(("space", "shell")), P("shell", "space"))
    return jax.shard_map(
        on_device, mesh=mesh, in_specs=in_specs, out_specs=out_specs, check_vma=False
    )
```

```python
import jax
import jax.numpy as jnp
from jax import lax
from jax.sharding import PartitionSpec as P
from jax.experimental import pallas as pl
from jax.experimental.pallas import tpu as pltpu

ITERS = 2
HI = lax.Precision.HIGHEST


def one_hot_pair(index, count):
    low_count = 64
    high_count = count // low_count
    flat = index.reshape(-1)
    high = (flat // low_count)[:, None] == lax.broadcasted_iota(jnp.int32, (1, high_count), 1)
    low = (flat % low_count)[:, None] == lax.broadcasted_iota(jnp.int32, (1, low_count), 1)
    return high.astype(jnp.float32), low.astype(jnp.float32)


def pick(table, high, low):
    rows = jnp.dot(high, table.reshape(high.shape[1], low.shape[1]), precision=HI)
    return jnp.sum(rows * low, axis=1)


def spread(values, high, low):
    return jnp.dot(high.T, values.reshape(-1)[:, None] * low, precision=HI).reshape(-1)


UNROLL = 8
ACCS = 4


def scatter_kernel(idx_ref, xs_ref, feat_ref, init_ref, out_ref, *accs):
    accs[0][...] = init_ref[...]
    for acc in accs[1:]:
        acc[...] = jnp.zeros(acc.shape, acc.dtype)

    def body(step, carry):
        for u in range(UNROLL):
            k = step * UNROLL + u
            acc = accs[u % ACCS]
            acc[pl.ds(idx_ref[k], 1), :] += xs_ref[k] * feat_ref[pl.ds(k, 1), :]
        return carry

    lax.fori_loop(0, feat_ref.shape[0] // UNROLL, body, 0)
    total = accs[0][...]
    for acc in accs[1:]:
        total = total + acc[...]
    out_ref[...] = total


def row_scatter(idx, xs, feat, init):
    smem = pl.BlockSpec(memory_space=pltpu.SMEM)
    vmem = pl.BlockSpec(memory_space=pltpu.VMEM)
    return pl.pallas_call(
        scatter_kernel,
        out_shape=jax.ShapeDtypeStruct(init.shape, jnp.float32),
        in_specs=[smem, smem, vmem, vmem],
        out_specs=vmem,
        scratch_shapes=[pltpu.VMEM(init.shape, jnp.float32) for _ in range(ACCS)],
    )(idx, xs, feat, init)


def gather_kernel(idx_ref, table_ref, feat_ref, out_ref, rows_ref):
    def body(step, carry):
        for u in range(UNROLL):
            k = step * UNROLL + u
            rows_ref[pl.ds(k, 1), :] = table_ref[pl.ds(idx_ref[k], 1), :]
        return carry

    lax.fori_loop(0, feat_ref.shape[0] // UNROLL, body, 0)
    lanes = out_ref.shape[1]

    def reduce_block(block, carry):
        start = pl.multiple_of(block * lanes, lanes)
        prod = rows_ref[pl.ds(start, lanes), :] * feat_ref[pl.ds(start, lanes), :]
        sums = lax.dot_general(
            jnp.ones((8, lanes), jnp.float32), prod, (((1,), (1,)), ((), ())),
            precision=HI, preferred_element_type=jnp.float32,
        )
        out_ref[pl.ds(block, 1), :] = sums[0:1, :]
        return carry

    lax.fori_loop(0, out_ref.shape[0], reduce_block, 0)


def row_gather_dot(idx, table, feat):
    smem = pl.BlockSpec(memory_space=pltpu.SMEM)
    vmem = pl.BlockSpec(memory_space=pltpu.VMEM)
    return pl.pallas_call(
        gather_kernel,
        out_shape=jax.ShapeDtypeStruct((feat.shape[0] // 128, 128), jnp.float32),
        in_specs=[smem, vmem, vmem],
        out_specs=vmem,
        scratch_shapes=[pltpu.VMEM(feat.shape, jnp.float32)],
    )(idx, table, feat)


def on_device(weights, seg_streamline, seg_features, pair_counts, seg_voxel, dictionary, measured):
    blocks = seg_streamline.shape[2]
    slots = seg_streamline.shape[3]
    coeffs = seg_features.shape[4]
    streams = weights.shape[0]
    stream_index = seg_streamline.reshape(blocks, slots)
    voxel_index = seg_voxel.reshape(blocks * slots)
    counts = pair_counts.reshape(blocks)
    live_slot = lax.broadcasted_iota(jnp.int32, (blocks, slots), 1) < counts[:, None]
    masked = jnp.where(
        live_slot[:, :, None], seg_features.reshape(blocks, slots, coeffs), jnp.float32(0.0)
    )
    half = slots // 2
    feat_parts = [
        lax.all_to_all(masked[:, h * half:(h + 1) * half], "space", 0, 0, tiled=True)
        for h in range(2)
    ]
    gram = lax.psum(jnp.dot(dictionary, dictionary.T, precision=HI), "shell")
    data_proj = lax.psum(jnp.dot(measured.T, dictionary.T, precision=HI), "shell")
    feat_parts[1], gram, data_proj = lax.optimization_barrier((feat_parts[1], gram, data_proj))
    vox_parts = [voxel_index.reshape(blocks, slots)[:, h * half:(h + 1) * half].reshape(-1)
                 for h in range(2)]
    local_feat = jnp.concatenate(feat_parts, axis=1).reshape(blocks * slots, coeffs)
    high, low = one_hot_pair(stream_index, streams)
    column_sq = spread(jnp.sum(masked * masked, axis=2), high, low)
    scaling = 0.5 / (0.5 + column_sq)
    current = weights
    residual = jnp.zeros(measured.shape, jnp.float32)
    for iteration in range(ITERS):
        picked = pick(current, high, low).reshape(blocks, slots)
        local_x = lax.all_to_all(picked, "space", split_axis=0, concat_axis=0, tiled=True)
        partial_coeff = jnp.zeros((measured.shape[1], coeffs), jnp.float32)
        if iteration == 0:
            for h in range(2):
                part_x = local_x[:, h * half:(h + 1) * half].reshape(-1)
                partial_coeff = row_scatter(
                    vox_parts[h], part_x, feat_parts[h].reshape(-1, coeffs), partial_coeff
                )
        else:
            partial_coeff = row_scatter(
                voxel_index, local_x.reshape(-1), local_feat, partial_coeff
            )
        coeff_sum = lax.psum(partial_coeff, "shell")
        if iteration == ITERS - 1:
            residual = (
                jnp.einsum("jg,vj->gv", dictionary, coeff_sum, precision=HI) - measured
            )
        adjoint = jnp.dot(coeff_sum, gram, precision=HI) - data_proj
        local_grad = row_gather_dot(voxel_index, adjoint, local_feat).reshape(blocks, slots)
        grad_slot = lax.all_to_all(local_grad, "space", split_axis=0, concat_axis=0, tiled=True)
        gradient = spread(grad_slot, high, low)
        current = jnp.maximum(current - scaling * gradient, 0.0)
    return (current, residual)


def solution(mesh):
    in_specs = (
        P(("space", "shell")),
        P("space", "shell", None, None),
        P("space", "shell", None, None, None),
        P("space", "shell", None),
        P("space", "shell", None, None),
        P(None, "shell"),
        P("shell", "space"),
    )
    out_specs = (P(("space", "shell")), P("shell", "space"))
    return jax.shard_map(
        on_device, mesh=mesh, in_specs=in_specs, out_specs=out_specs, check_vma=False
    )
```

```python
import functools

import jax
import jax.numpy as jnp
from jax import lax
from jax.sharding import PartitionSpec as P
from jax.experimental import pallas as pl
from jax.experimental.pallas import tpu as pltpu

ITERS = 2
HI = lax.Precision.HIGHEST


def one_hot_pair(index, count):
    low_count = 64
    high_count = count // low_count
    flat = index.reshape(-1)
    high = (flat // low_count)[:, None] == lax.broadcasted_iota(jnp.int32, (1, high_count), 1)
    low = (flat % low_count)[:, None] == lax.broadcasted_iota(jnp.int32, (1, low_count), 1)
    return high.astype(jnp.float32), low.astype(jnp.float32)


def pick(table, high, low):
    rows = jnp.dot(high, table.reshape(high.shape[1], low.shape[1]), precision=HI)
    return jnp.sum(rows * low, axis=1)


def spread(values, high, low):
    return jnp.dot(high.T, values.reshape(-1)[:, None] * low, precision=HI).reshape(-1)


UNROLL = 8
ACCS = 4


def scatter_kernel(slots, pad, idx_ref, xs_ref, feat_ref, init_ref, out_ref, *accs):
    accs[0][...] = init_ref[...]
    for acc in accs[1:]:
        acc[...] = jnp.zeros(acc.shape, acc.dtype)

    def body(step, carry):
        for u in range(UNROLL):
            k = step * UNROLL + u
            acc = accs[u % ACCS]
            row = k + (k // slots) * pad
            acc[pl.ds(idx_ref[k], 1), :] += xs_ref[k] * feat_ref[pl.ds(row, 1), :]
        return carry

    lax.fori_loop(0, idx_ref.shape[0] // UNROLL, body, 0)
    total = accs[0][...]
    for acc in accs[1:]:
        total = total + acc[...]
    out_ref[...] = total


def row_scatter(idx, xs, feat, init, slots, pad):
    smem = pl.BlockSpec(memory_space=pltpu.SMEM)
    vmem = pl.BlockSpec(memory_space=pltpu.VMEM)
    return pl.pallas_call(
        functools.partial(scatter_kernel, slots, pad),
        out_shape=jax.ShapeDtypeStruct(init.shape, jnp.float32),
        in_specs=[smem, smem, vmem, vmem],
        out_specs=vmem,
        scratch_shapes=[pltpu.VMEM(init.shape, jnp.float32) for _ in range(ACCS)],
    )(idx, xs, feat, init)


def gather_kernel(slots, pad, idx_ref, table_ref, feat_ref, out_ref, rows_ref):
    def body(step, carry):
        for u in range(UNROLL):
            k = step * UNROLL + u
            rows_ref[pl.ds(k, 1), :] = table_ref[pl.ds(idx_ref[k], 1), :]
        return carry

    lax.fori_loop(0, idx_ref.shape[0] // UNROLL, body, 0)
    lanes = out_ref.shape[1]

    def reduce_block(block, carry):
        start = pl.multiple_of(block * lanes, lanes)
        frow = pl.multiple_of(start + (start // slots) * pad, 8)
        prod = rows_ref[pl.ds(start, lanes), :] * feat_ref[pl.ds(frow, lanes), :]
        out_ref[pl.ds(block, 1), :] = jnp.sum(prod.T, axis=0, keepdims=True)
        return carry

    lax.fori_loop(0, out_ref.shape[0], reduce_block, 0)


def row_gather_dot(idx, table, feat, slots, pad):
    smem = pl.BlockSpec(memory_space=pltpu.SMEM)
    vmem = pl.BlockSpec(memory_space=pltpu.VMEM)
    return pl.pallas_call(
        functools.partial(gather_kernel, slots, pad),
        out_shape=jax.ShapeDtypeStruct((idx.shape[0] // 128, 128), jnp.float32),
        in_specs=[smem, vmem, vmem],
        out_specs=vmem,
        scratch_shapes=[pltpu.VMEM((idx.shape[0], feat.shape[1]), jnp.float32)],
    )(idx, table, feat)


def on_device(weights, seg_streamline, seg_features, pair_counts, seg_voxel, dictionary, measured):
    blocks = seg_streamline.shape[2]
    slots = seg_streamline.shape[3]
    coeffs = seg_features.shape[4]
    streams = weights.shape[0]
    stream_index = seg_streamline.reshape(blocks, slots)
    voxel_index = seg_voxel.reshape(blocks * slots)
    counts = pair_counts.reshape(blocks)
    live_slot = lax.broadcasted_iota(jnp.int32, (blocks, slots), 1) < counts[:, None]
    masked = jnp.where(
        live_slot[:, :, None], seg_features.reshape(blocks, slots, coeffs), jnp.float32(0.0)
    )
    high, low = one_hot_pair(stream_index, streams)
    column_sq = spread(jnp.sum(masked * masked, axis=2), high, low)
    scaling = 0.5 / (0.5 + column_sq)
    pad = 8
    picked = pick(weights, high, low).reshape(blocks, slots // coeffs, coeffs)
    payload = jnp.concatenate(
        [masked, picked, jnp.zeros((blocks, pad - slots // coeffs, coeffs), jnp.float32)], axis=1
    )
    received = lax.all_to_all(payload, "space", 0, 0, tiled=True)
    gram = lax.psum(jnp.dot(dictionary, dictionary.T, precision=HI), "shell")
    data_proj = lax.psum(jnp.dot(measured.T, dictionary.T, precision=HI), "shell")
    received, gram, data_proj = lax.optimization_barrier((received, gram, data_proj))
    local_x = received[:, slots:slots + slots // coeffs].reshape(blocks, slots)
    local_feat = received.reshape(blocks * (slots + pad), coeffs)
    current = weights
    residual = jnp.zeros(measured.shape, jnp.float32)
    for iteration in range(ITERS):
        if iteration > 0:
            picked = pick(current, high, low).reshape(blocks, slots)
            local_x = lax.all_to_all(picked, "space", split_axis=0, concat_axis=0, tiled=True)
        partial_coeff = row_scatter(
            voxel_index, local_x.reshape(-1), local_feat,
            jnp.zeros((measured.shape[1], coeffs), jnp.float32), slots, pad,
        )
        coeff_sum = lax.psum(partial_coeff, "shell")
        if iteration == ITERS - 1:
            residual = (
                jnp.einsum("jg,vj->gv", dictionary, coeff_sum, precision=HI) - measured
            )
        adjoint = jnp.dot(coeff_sum, gram, precision=HI) - data_proj
        local_grad = row_gather_dot(voxel_index, adjoint, local_feat, slots, pad)
        grad_slot = lax.all_to_all(
            local_grad.reshape(blocks, slots), "space", split_axis=0, concat_axis=0, tiled=True
        )
        gradient = spread(grad_slot, high, low)
        current = jnp.maximum(current - scaling * gradient, 0.0)
    return (current, residual)


def solution(mesh):
    in_specs = (
        P(("space", "shell")),
        P("space", "shell", None, None),
        P("space", "shell", None, None, None),
        P("space", "shell", None),
        P("space", "shell", None, None),
        P(None, "shell"),
        P("shell", "space"),
    )
    out_specs = (P(("space", "shell")), P("shell", "space"))
    return jax.shard_map(
        on_device, mesh=mesh, in_specs=in_specs, out_specs=out_specs, check_vma=False
    )
```

```python
import jax
import jax.numpy as jnp
from jax import lax
from jax.sharding import PartitionSpec as P
from jax.experimental import pallas as pl
from jax.experimental.pallas import tpu as pltpu

ITERS = 2
HI = lax.Precision.HIGHEST


def one_hot_pair(index, count):
    low_count = 64
    high_count = count // low_count
    flat = index.reshape(-1)
    high = (flat // low_count)[:, None] == lax.broadcasted_iota(jnp.int32, (1, high_count), 1)
    low = (flat % low_count)[:, None] == lax.broadcasted_iota(jnp.int32, (1, low_count), 1)
    return high.astype(jnp.float32), low.astype(jnp.float32)


def pick(table, high, low):
    rows = jnp.dot(high, table.reshape(high.shape[1], low.shape[1]), precision=HI)
    return jnp.sum(rows * low, axis=1)


def spread(values, high, low):
    return jnp.dot(high.T, values.reshape(-1)[:, None] * low, precision=HI).reshape(-1)


UNROLL = 8
ACCS = 4


def scatter_kernel(idx_ref, xs_ref, feat_ref, init_ref, out_ref, *accs):
    accs[0][...] = init_ref[...]
    for acc in accs[1:]:
        acc[...] = jnp.zeros(acc.shape, acc.dtype)

    def body(step, carry):
        for u in range(UNROLL):
            k = step * UNROLL + u
            acc = accs[u % ACCS]
            acc[pl.ds(idx_ref[k], 1), :] += xs_ref[k] * feat_ref[pl.ds(k, 1), :]
        return carry

    lax.fori_loop(0, feat_ref.shape[0] // UNROLL, body, 0)
    total = accs[0][...]
    for acc in accs[1:]:
        total = total + acc[...]
    out_ref[...] = total


def row_scatter(idx, xs, feat, init):
    smem = pl.BlockSpec(memory_space=pltpu.SMEM)
    vmem = pl.BlockSpec(memory_space=pltpu.VMEM)
    return pl.pallas_call(
        scatter_kernel,
        out_shape=jax.ShapeDtypeStruct(init.shape, jnp.float32),
        in_specs=[smem, smem, vmem, vmem],
        out_specs=vmem,
        scratch_shapes=[pltpu.VMEM(init.shape, jnp.float32) for _ in range(ACCS)],
    )(idx, xs, feat, init)


def gather_kernel(idx_ref, table_ref, feat_ref, out_ref, rows_ref):
    def body(step, carry):
        for u in range(UNROLL):
            k = step * UNROLL + u
            rows_ref[pl.ds(k, 1), :] = table_ref[pl.ds(idx_ref[k], 1), :]
        return carry

    lax.fori_loop(0, feat_ref.shape[0] // UNROLL, body, 0)
    lanes = out_ref.shape[1]

    def reduce_block(block, carry):
        start = pl.multiple_of(block * lanes, lanes)
        prod = rows_ref[pl.ds(start, lanes), :] * feat_ref[pl.ds(start, lanes), :]
        out_ref[pl.ds(block, 1), :] = jnp.sum(prod.T, axis=0, keepdims=True)
        return carry

    lax.fori_loop(0, out_ref.shape[0], reduce_block, 0)


def row_gather_dot(idx, table, feat):
    smem = pl.BlockSpec(memory_space=pltpu.SMEM)
    vmem = pl.BlockSpec(memory_space=pltpu.VMEM)
    return pl.pallas_call(
        gather_kernel,
        out_shape=jax.ShapeDtypeStruct((feat.shape[0] // 128, 128), jnp.float32),
        in_specs=[smem, vmem, vmem],
        out_specs=vmem,
        scratch_shapes=[pltpu.VMEM(feat.shape, jnp.float32)],
    )(idx, table, feat)


def on_device(weights, seg_streamline, seg_features, pair_counts, seg_voxel, dictionary, measured):
    blocks = seg_streamline.shape[2]
    slots = seg_streamline.shape[3]
    coeffs = seg_features.shape[4]
    streams = weights.shape[0]
    stream_index = seg_streamline.reshape(blocks, slots)
    voxel_index = seg_voxel.reshape(blocks * slots)
    counts = pair_counts.reshape(blocks)
    live_slot = lax.broadcasted_iota(jnp.int32, (blocks, slots), 1) < counts[:, None]
    masked = jnp.where(
        live_slot[:, :, None], seg_features.reshape(blocks, slots, coeffs), jnp.float32(0.0)
    )
    half = slots // 2
    feat_parts = [
        lax.all_to_all(masked[:, h * half:(h + 1) * half], "space", 0, 0, tiled=True)
        for h in range(2)
    ]
    gram = lax.psum(jnp.dot(dictionary, dictionary.T, precision=HI), "shell")
    data_proj = lax.psum(jnp.dot(measured.T, dictionary.T, precision=HI), "shell")
    feat_parts[1], gram, data_proj = lax.optimization_barrier((feat_parts[1], gram, data_proj))
    vox_parts = [voxel_index.reshape(blocks, slots)[:, h * half:(h + 1) * half].reshape(-1)
                 for h in range(2)]
    local_feat = jnp.concatenate(feat_parts, axis=1).reshape(blocks * slots, coeffs)
    high, low = one_hot_pair(stream_index, streams)
    column_sq = spread(jnp.sum(masked * masked, axis=2), high, low)
    scaling = 0.5 / (0.5 + column_sq)
    current = weights
    residual = jnp.zeros(measured.shape, jnp.float32)
    for iteration in range(ITERS):
        picked = pick(current, high, low).reshape(blocks, slots)
        local_x = lax.all_to_all(picked, "space", split_axis=0, concat_axis=0, tiled=True)
        partial_coeff = jnp.zeros((measured.shape[1], coeffs), jnp.float32)
        if iteration == 0:
            for h in range(2):
                part_x = local_x[:, h * half:(h + 1) * half].reshape(-1)
                partial_coeff = row_scatter(
                    vox_parts[h], part_x, feat_parts[h].reshape(-1, coeffs), partial_coeff
                )
        else:
            partial_coeff = row_scatter(
                voxel_index, local_x.reshape(-1), local_feat, partial_coeff
            )
        coeff_sum = lax.psum(partial_coeff, "shell")
        if iteration == ITERS - 1:
            residual = (
                jnp.einsum("jg,vj->gv", dictionary, coeff_sum, precision=HI) - measured
            )
        adjoint = jnp.dot(coeff_sum, gram, precision=lax.Precision.HIGH) - data_proj
        local_grad = row_gather_dot(voxel_index, adjoint, local_feat).reshape(blocks, slots)
        grad_slot = lax.all_to_all(local_grad, "space", split_axis=0, concat_axis=0, tiled=True)
        gradient = spread(grad_slot, high, low)
        current = jnp.maximum(current - scaling * gradient, 0.0)
    return (current, residual)


def solution(mesh):
    in_specs = (
        P(("space", "shell")),
        P("space", "shell", None, None),
        P("space", "shell", None, None, None),
        P("space", "shell", None),
        P("space", "shell", None, None),
        P(None, "shell"),
        P("shell", "space"),
    )
    out_specs = (P(("space", "shell")), P("shell", "space"))
    return jax.shard_map(
        on_device, mesh=mesh, in_specs=in_specs, out_specs=out_specs, check_vma=False
    )
```

```python
import jax
import jax.numpy as jnp
from jax import lax
from jax.sharding import PartitionSpec as P
from jax.experimental import pallas as pl
from jax.experimental.pallas import tpu as pltpu

ITERS = 2
HI = lax.Precision.HIGHEST


def one_hot_pair(index, count):
    low_count = 64
    high_count = count // low_count
    flat = index.reshape(-1)
    high = (flat // low_count)[:, None] == lax.broadcasted_iota(jnp.int32, (1, high_count), 1)
    low = (flat % low_count)[:, None] == lax.broadcasted_iota(jnp.int32, (1, low_count), 1)
    return high.astype(jnp.float32), low.astype(jnp.float32)


def pick(table, high, low):
    rows = jnp.dot(high, table.reshape(high.shape[1], low.shape[1]), precision=HI)
    return jnp.sum(rows * low, axis=1)


def spread(values, high, low):
    return jnp.dot(high.T, values.reshape(-1)[:, None] * low, precision=HI).reshape(-1)


UNROLL = 64
ACCS = 8


def scatter_kernel(idx_ref, xs_ref, feat_ref, init_ref, out_ref, *accs):
    accs[0][...] = init_ref[...]
    for acc in accs[1:]:
        acc[...] = jnp.zeros(acc.shape, acc.dtype)

    def body(step, carry):
        for u in range(UNROLL):
            k = step * UNROLL + u
            acc = accs[u % ACCS]
            acc[pl.ds(idx_ref[k], 1), :] += xs_ref[k] * feat_ref[pl.ds(k, 1), :]
        return carry

    lax.fori_loop(0, feat_ref.shape[0] // UNROLL, body, 0)
    total = accs[0][...]
    for acc in accs[1:]:
        total = total + acc[...]
    out_ref[...] = total


def row_scatter(idx, xs, feat, init):
    smem = pl.BlockSpec(memory_space=pltpu.SMEM)
    vmem = pl.BlockSpec(memory_space=pltpu.VMEM)
    return pl.pallas_call(
        scatter_kernel,
        out_shape=jax.ShapeDtypeStruct(init.shape, jnp.float32),
        in_specs=[smem, smem, vmem, vmem],
        out_specs=vmem,
        scratch_shapes=[pltpu.VMEM(init.shape, jnp.float32) for _ in range(ACCS)],
    )(idx, xs, feat, init)


def gather_kernel(idx_ref, table_ref, feat_ref, out_ref, rows_ref):
    def body(step, carry):
        for u in range(UNROLL):
            k = step * UNROLL + u
            rows_ref[pl.ds(k, 1), :] = table_ref[pl.ds(idx_ref[k], 1), :]
        return carry

    lax.fori_loop(0, feat_ref.shape[0] // UNROLL, body, 0)
    lanes = out_ref.shape[1]

    def reduce_block(block, carry):
        start = pl.multiple_of(block * lanes, lanes)
        prod = rows_ref[pl.ds(start, lanes), :] * feat_ref[pl.ds(start, lanes), :]
        out_ref[pl.ds(block, 1), :] = jnp.sum(prod.T, axis=0, keepdims=True)
        return carry

    lax.fori_loop(0, out_ref.shape[0], reduce_block, 0)


def row_gather_dot(idx, table, feat):
    smem = pl.BlockSpec(memory_space=pltpu.SMEM)
    vmem = pl.BlockSpec(memory_space=pltpu.VMEM)
    return pl.pallas_call(
        gather_kernel,
        out_shape=jax.ShapeDtypeStruct((feat.shape[0] // 128, 128), jnp.float32),
        in_specs=[smem, vmem, vmem],
        out_specs=vmem,
        scratch_shapes=[pltpu.VMEM(feat.shape, jnp.float32)],
    )(idx, table, feat)


def on_device(weights, seg_streamline, seg_features, pair_counts, seg_voxel, dictionary, measured):
    blocks = seg_streamline.shape[2]
    slots = seg_streamline.shape[3]
    coeffs = seg_features.shape[4]
    streams = weights.shape[0]
    stream_index = seg_streamline.reshape(blocks, slots)
    voxel_index = seg_voxel.reshape(blocks * slots)
    counts = pair_counts.reshape(blocks)
    live_slot = lax.broadcasted_iota(jnp.int32, (blocks, slots), 1) < counts[:, None]
    masked = jnp.where(
        live_slot[:, :, None], seg_features.reshape(blocks, slots, coeffs), jnp.float32(0.0)
    )
    half = slots // 2
    feat_parts = [
        lax.all_to_all(masked[:, h * half:(h + 1) * half], "space", 0, 0, tiled=True)
        for h in range(2)
    ]
    gram = lax.psum(jnp.dot(dictionary, dictionary.T, precision=HI), "shell")
    data_proj = lax.psum(jnp.dot(measured.T, dictionary.T, precision=HI), "shell")
    feat_parts[1], gram, data_proj = lax.optimization_barrier((feat_parts[1], gram, data_proj))
    vox_parts = [voxel_index.reshape(blocks, slots)[:, h * half:(h + 1) * half].reshape(-1)
                 for h in range(2)]
    local_feat = jnp.concatenate(feat_parts, axis=1).reshape(blocks * slots, coeffs)
    high, low = one_hot_pair(stream_index, streams)
    column_sq = spread(jnp.sum(masked * masked, axis=2), high, low)
    scaling = 0.5 / (0.5 + column_sq)
    current = weights
    residual = jnp.zeros(measured.shape, jnp.float32)
    for iteration in range(ITERS):
        picked = pick(current, high, low).reshape(blocks, slots)
        local_x = lax.all_to_all(picked, "space", split_axis=0, concat_axis=0, tiled=True)
        partial_coeff = jnp.zeros((measured.shape[1], coeffs), jnp.float32)
        if iteration == 0:
            for h in range(2):
                part_x = local_x[:, h * half:(h + 1) * half].reshape(-1)
                partial_coeff = row_scatter(
                    vox_parts[h], part_x, feat_parts[h].reshape(-1, coeffs), partial_coeff
                )
        else:
            partial_coeff = row_scatter(
                voxel_index, local_x.reshape(-1), local_feat, partial_coeff
            )
        coeff_sum = lax.psum(partial_coeff, "shell")
        if iteration == ITERS - 1:
            residual = (
                jnp.einsum("jg,vj->gv", dictionary, coeff_sum, precision=HI) - measured
            )
        adjoint = jnp.dot(coeff_sum, gram, precision=HI) - data_proj
        local_grad = row_gather_dot(voxel_index, adjoint, local_feat).reshape(blocks, slots)
        grad_slot = lax.all_to_all(local_grad, "space", split_axis=0, concat_axis=0, tiled=True)
        gradient = spread(grad_slot, high, low)
        current = jnp.maximum(current - scaling * gradient, 0.0)
    return (current, residual)


def solution(mesh):
    in_specs = (
        P(("space", "shell")),
        P("space", "shell", None, None),
        P("space", "shell", None, None, None),
        P("space", "shell", None),
        P("space", "shell", None, None),
        P(None, "shell"),
        P("shell", "space"),
    )
    out_specs = (P(("space", "shell")), P("shell", "space"))
    return jax.shard_map(
        on_device, mesh=mesh, in_specs=in_specs, out_specs=out_specs, check_vma=False
    )
```

```python
import jax
import jax.numpy as jnp
from jax import lax
from jax.sharding import PartitionSpec as P
from jax.experimental import pallas as pl
from jax.experimental.pallas import tpu as pltpu

ITERS = 2
HI = lax.Precision.HIGHEST


def one_hot_pair(index, count):
    low_count = 64
    high_count = count // low_count
    flat = index.reshape(-1)
    high = (flat // low_count)[:, None] == lax.broadcasted_iota(jnp.int32, (1, high_count), 1)
    low = (flat % low_count)[:, None] == lax.broadcasted_iota(jnp.int32, (1, low_count), 1)
    return high.astype(jnp.float32), low.astype(jnp.float32)


def pick(table, high, low):
    rows = jnp.dot(high, table.reshape(high.shape[1], low.shape[1]), precision=HI)
    return jnp.sum(rows * low, axis=1)


def spread(values, high, low):
    return jnp.dot(high.T, values.reshape(-1)[:, None] * low, precision=HI).reshape(-1)


UNROLL = 64
ACCS = 8


def scatter_kernel(idx_ref, xs_ref, feat_ref, init_ref, out_ref, *accs):
    accs[0][...] = init_ref[...]
    for acc in accs[1:]:
        acc[...] = jnp.zeros(acc.shape, acc.dtype)

    def body(step, carry):
        for u in range(UNROLL):
            k = step * UNROLL + u
            acc = accs[u % ACCS]
            acc[pl.ds(idx_ref[k], 1), :] += xs_ref[k] * feat_ref[pl.ds(k, 1), :]
        return carry

    lax.fori_loop(0, feat_ref.shape[0] // UNROLL, body, 0)
    total = accs[0][...]
    for acc in accs[1:]:
        total = total + acc[...]
    out_ref[...] = total


def row_scatter(idx, xs, feat, init):
    smem = pl.BlockSpec(memory_space=pltpu.SMEM)
    vmem = pl.BlockSpec(memory_space=pltpu.VMEM)
    return pl.pallas_call(
        scatter_kernel,
        out_shape=jax.ShapeDtypeStruct(init.shape, jnp.float32),
        in_specs=[smem, smem, vmem, vmem],
        out_specs=vmem,
        scratch_shapes=[pltpu.VMEM(init.shape, jnp.float32) for _ in range(ACCS)],
    )(idx, xs, feat, init)


def gather_kernel(idx_ref, table_ref, feat_ref, out_ref, rows_ref):
    def body(step, carry):
        for u in range(UNROLL):
            k = step * UNROLL + u
            rows_ref[pl.ds(k, 1), :] = table_ref[pl.ds(idx_ref[k], 1), :]
        return carry

    lax.fori_loop(0, feat_ref.shape[0] // UNROLL, body, 0)
    lanes = feat_ref.shape[1]
    chunk = out_ref.shape[1]
    ones = jnp.ones((8, lanes), jnp.bfloat16)

    def reduce_chunk(c, carry):
        start = pl.multiple_of(c * chunk, chunk)
        prod = rows_ref[pl.ds(start, chunk), :] * feat_ref[pl.ds(start, chunk), :]
        sums = jnp.zeros((8, chunk), jnp.float32)
        for _ in range(3):
            part = prod.astype(jnp.bfloat16)
            prod = prod - part.astype(jnp.float32)
            sums = sums + lax.dot_general(
                ones, part, (((1,), (1,)), ((), ())), preferred_element_type=jnp.float32
            )
        out_ref[pl.ds(c, 1), :] = sums[0:1, :]
        return carry

    lax.fori_loop(0, out_ref.shape[0], reduce_chunk, 0)


def row_gather_dot(idx, table, feat):
    smem = pl.BlockSpec(memory_space=pltpu.SMEM)
    vmem = pl.BlockSpec(memory_space=pltpu.VMEM)
    return pl.pallas_call(
        gather_kernel,
        out_shape=jax.ShapeDtypeStruct((8, feat.shape[0] // 8), jnp.float32),
        in_specs=[smem, vmem, vmem],
        out_specs=vmem,
        scratch_shapes=[pltpu.VMEM(feat.shape, jnp.float32)],
    )(idx, table, feat)


def on_device(weights, seg_streamline, seg_features, pair_counts, seg_voxel, dictionary, measured):
    blocks = seg_streamline.shape[2]
    slots = seg_streamline.shape[3]
    coeffs = seg_features.shape[4]
    streams = weights.shape[0]
    stream_index = seg_streamline.reshape(blocks, slots)
    voxel_index = seg_voxel.reshape(blocks * slots)
    counts = pair_counts.reshape(blocks)
    live_slot = lax.broadcasted_iota(jnp.int32, (blocks, slots), 1) < counts[:, None]
    masked = jnp.where(
        live_slot[:, :, None], seg_features.reshape(blocks, slots, coeffs), jnp.float32(0.0)
    )
    half = slots // 2
    feat_parts = [
        lax.all_to_all(masked[:, h * half:(h + 1) * half], "space", 0, 0, tiled=True)
        for h in range(2)
    ]
    gram = lax.psum(jnp.dot(dictionary, dictionary.T, precision=HI), "shell")
    data_proj = lax.psum(jnp.dot(measured.T, dictionary.T, precision=HI), "shell")
    feat_parts[1], gram, data_proj = lax.optimization_barrier((feat_parts[1], gram, data_proj))
    vox_parts = [voxel_index.reshape(blocks, slots)[:, h * half:(h + 1) * half].reshape(-1)
                 for h in range(2)]
    local_feat = jnp.concatenate(feat_parts, axis=1).reshape(blocks * slots, coeffs)
    high, low = one_hot_pair(stream_index, streams)
    column_sq = spread(jnp.sum(masked * masked, axis=2), high, low)
    scaling = 0.5 / (0.5 + column_sq)
    current = weights
    residual = jnp.zeros(measured.shape, jnp.float32)
    for iteration in range(ITERS):
        picked = pick(current, high, low).reshape(blocks, slots)
        local_x = lax.all_to_all(picked, "space", split_axis=0, concat_axis=0, tiled=True)
        partial_coeff = jnp.zeros((measured.shape[1], coeffs), jnp.float32)
        if iteration == 0:
            for h in range(2):
                part_x = local_x[:, h * half:(h + 1) * half].reshape(-1)
                partial_coeff = row_scatter(
                    vox_parts[h], part_x, feat_parts[h].reshape(-1, coeffs), partial_coeff
                )
        else:
            partial_coeff = row_scatter(
                voxel_index, local_x.reshape(-1), local_feat, partial_coeff
            )
        coeff_sum = lax.psum(partial_coeff, "shell")
        if iteration == ITERS - 1:
            residual = (
                jnp.einsum("jg,vj->gv", dictionary, coeff_sum, precision=HI) - measured
            )
        adjoint = jnp.dot(coeff_sum, gram, precision=HI) - data_proj
        local_grad = row_gather_dot(voxel_index, adjoint, local_feat).reshape(blocks, slots)
        grad_slot = lax.all_to_all(local_grad, "space", split_axis=0, concat_axis=0, tiled=True)
        gradient = spread(grad_slot, high, low)
        current = jnp.maximum(current - scaling * gradient, 0.0)
    return (current, residual)


def solution(mesh):
    in_specs = (
        P(("space", "shell")),
        P("space", "shell", None, None),
        P("space", "shell", None, None, None),
        P("space", "shell", None),
        P("space", "shell", None, None),
        P(None, "shell"),
        P("shell", "space"),
    )
    out_specs = (P(("space", "shell")), P("shell", "space"))
    return jax.shard_map(
        on_device, mesh=mesh, in_specs=in_specs, out_specs=out_specs, check_vma=False
    )
```

```python
import functools

import jax
import jax.numpy as jnp
from jax import lax
from jax.sharding import PartitionSpec as P
from jax.experimental import pallas as pl
from jax.experimental.pallas import tpu as pltpu

ITERS = 2
HI = lax.Precision.HIGHEST


def one_hot_pair(index, count):
    low_count = 64
    high_count = count // low_count
    flat = index.reshape(-1)
    high = (flat // low_count)[:, None] == lax.broadcasted_iota(jnp.int32, (1, high_count), 1)
    low = (flat % low_count)[:, None] == lax.broadcasted_iota(jnp.int32, (1, low_count), 1)
    return high.astype(jnp.float32), low.astype(jnp.float32)


def pick(table, high, low):
    rows = jnp.dot(high, table.reshape(high.shape[1], low.shape[1]), precision=HI)
    return jnp.sum(rows * low, axis=1)


def spread(values, high, low):
    return jnp.dot(high.T, values.reshape(-1)[:, None] * low, precision=HI).reshape(-1)


UNROLL = 64
ACCS = 8


def scatter_kernel(slots, pad, idx_ref, xs_ref, feat_ref, init_ref, out_ref, *accs):
    accs[0][...] = init_ref[...]
    for acc in accs[1:]:
        acc[...] = jnp.zeros(acc.shape, acc.dtype)

    def body(step, carry):
        row = step * UNROLL
        if pad:
            row = row + (row // slots) * pad
        for u in range(UNROLL):
            k = step * UNROLL + u
            acc = accs[u % ACCS]
            acc[pl.ds(idx_ref[k], 1), :] += xs_ref[k] * feat_ref[pl.ds(row + u, 1), :]
        return carry

    lax.fori_loop(0, idx_ref.shape[0] // UNROLL, body, 0)
    total = accs[0][...]
    for acc in accs[1:]:
        total = total + acc[...]
    out_ref[...] = total


def row_scatter(idx, xs, feat, init, slots=128, pad=0):
    smem = pl.BlockSpec(memory_space=pltpu.SMEM)
    vmem = pl.BlockSpec(memory_space=pltpu.VMEM)
    return pl.pallas_call(
        functools.partial(scatter_kernel, slots, pad),
        out_shape=jax.ShapeDtypeStruct(init.shape, jnp.float32),
        in_specs=[smem, smem, vmem, vmem],
        out_specs=vmem,
        scratch_shapes=[pltpu.VMEM(init.shape, jnp.float32) for _ in range(ACCS)],
    )(idx, xs, feat, init)


def gather_kernel(idx_ref, table_ref, feat_ref, out_ref, rows_ref):
    def body(step, carry):
        for u in range(UNROLL):
            k = step * UNROLL + u
            rows_ref[pl.ds(k, 1), :] = table_ref[pl.ds(idx_ref[k], 1), :]
        return carry

    lax.fori_loop(0, feat_ref.shape[0] // UNROLL, body, 0)
    lanes = feat_ref.shape[1]
    chunk = out_ref.shape[1]
    ones = jnp.ones((8, lanes), jnp.bfloat16)

    def reduce_chunk(c, carry):
        start = pl.multiple_of(c * chunk, chunk)
        prod = rows_ref[pl.ds(start, chunk), :] * feat_ref[pl.ds(start, chunk), :]
        sums = jnp.zeros((8, chunk), jnp.float32)
        for _ in range(3):
            part = prod.astype(jnp.bfloat16)
            prod = prod - part.astype(jnp.float32)
            sums = sums + lax.dot_general(
                ones, part, (((1,), (1,)), ((), ())), preferred_element_type=jnp.float32
            )
        out_ref[pl.ds(c, 1), :] = sums[0:1, :]
        return carry

    lax.fori_loop(0, out_ref.shape[0], reduce_chunk, 0)


def row_gather_dot(idx, table, feat):
    smem = pl.BlockSpec(memory_space=pltpu.SMEM)
    vmem = pl.BlockSpec(memory_space=pltpu.VMEM)
    return pl.pallas_call(
        gather_kernel,
        out_shape=jax.ShapeDtypeStruct((8, feat.shape[0] // 8), jnp.float32),
        in_specs=[smem, vmem, vmem],
        out_specs=vmem,
        scratch_shapes=[pltpu.VMEM(feat.shape, jnp.float32)],
    )(idx, table, feat)


def on_device(weights, seg_streamline, seg_features, pair_counts, seg_voxel, dictionary, measured):
    blocks = seg_streamline.shape[2]
    slots = seg_streamline.shape[3]
    coeffs = seg_features.shape[4]
    streams = weights.shape[0]
    stream_index = seg_streamline.reshape(blocks, slots)
    voxel_index = seg_voxel.reshape(blocks * slots)
    counts = pair_counts.reshape(blocks)
    live_slot = lax.broadcasted_iota(jnp.int32, (blocks, slots), 1) < counts[:, None]
    masked = jnp.where(
        live_slot[:, :, None], seg_features.reshape(blocks, slots, coeffs), jnp.float32(0.0)
    )
    high, low = one_hot_pair(stream_index, streams)
    column_sq = spread(jnp.sum(masked * masked, axis=2), high, low)
    scaling = 0.5 / (0.5 + column_sq)
    half = slots // 2
    pad = 8
    picked = pick(weights, high, low).reshape(blocks, slots // coeffs, coeffs)
    first = jnp.concatenate(
        [masked[:, :half], picked, jnp.zeros((blocks, pad - slots // coeffs, coeffs), jnp.float32)],
        axis=1,
    )
    first = lax.all_to_all(first, "space", 0, 0, tiled=True)
    second = lax.all_to_all(masked[:, half:], "space", 0, 0, tiled=True)
    gram = lax.psum(jnp.dot(dictionary, dictionary.T, precision=HI), "shell")
    data_proj = lax.psum(jnp.dot(measured.T, dictionary.T, precision=HI), "shell")
    second, gram, data_proj = lax.optimization_barrier((second, gram, data_proj))
    first_x = first[:, half:half + slots // coeffs].reshape(blocks, slots)
    vox_parts = [voxel_index.reshape(blocks, slots)[:, h * half:(h + 1) * half].reshape(-1)
                 for h in range(2)]
    local_feat = jnp.concatenate([first[:, :half], second], axis=1).reshape(blocks * slots, coeffs)
    current = weights
    residual = jnp.zeros(measured.shape, jnp.float32)
    for iteration in range(ITERS):
        partial_coeff = jnp.zeros((measured.shape[1], coeffs), jnp.float32)
        if iteration == 0:
            partial_coeff = row_scatter(
                vox_parts[0], first_x[:, :half].reshape(-1),
                first.reshape(-1, coeffs), partial_coeff, half, pad,
            )
            partial_coeff = row_scatter(
                vox_parts[1], first_x[:, half:].reshape(-1),
                second.reshape(-1, coeffs), partial_coeff,
            )
        else:
            picked = pick(current, high, low).reshape(blocks, slots)
            local_x = lax.all_to_all(picked, "space", split_axis=0, concat_axis=0, tiled=True)
            partial_coeff = row_scatter(
                voxel_index, local_x.reshape(-1), local_feat, partial_coeff
            )
        coeff_sum = lax.psum(partial_coeff, "shell")
        if iteration == ITERS - 1:
            residual = (
                jnp.einsum("jg,vj->gv", dictionary, coeff_sum, precision=HI) - measured
            )
        adjoint = jnp.dot(coeff_sum, gram, precision=HI) - data_proj
        local_grad = row_gather_dot(voxel_index, adjoint, local_feat).reshape(blocks, slots)
        grad_slot = lax.all_to_all(local_grad, "space", split_axis=0, concat_axis=0, tiled=True)
        gradient = spread(grad_slot, high, low)
        current = jnp.maximum(current - scaling * gradient, 0.0)
    return (current, residual)


def solution(mesh):
    in_specs = (
        P(("space", "shell")),
        P("space", "shell", None, None),
        P("space", "shell", None, None, None),
        P("space", "shell", None),
        P("space", "shell", None, None),
        P(None, "shell"),
        P("shell", "space"),
    )
    out_specs = (P(("space", "shell")), P("shell", "space"))
    return jax.shard_map(
        on_device, mesh=mesh, in_specs=in_specs, out_specs=out_specs, check_vma=False
    )
```

```python
import functools

import jax
import jax.numpy as jnp
from jax import lax
from jax.sharding import PartitionSpec as P
from jax.experimental import pallas as pl
from jax.experimental.pallas import tpu as pltpu

ITERS = 2
HI = lax.Precision.HIGHEST


def one_hot_pair(index, count):
    low_count = 64
    high_count = count // low_count
    flat = index.reshape(-1)
    high = (flat // low_count)[:, None] == lax.broadcasted_iota(jnp.int32, (1, high_count), 1)
    low = (flat % low_count)[:, None] == lax.broadcasted_iota(jnp.int32, (1, low_count), 1)
    return high.astype(jnp.float32), low.astype(jnp.float32)


def pick(table, high, low):
    rows = jnp.dot(high, table.reshape(high.shape[1], low.shape[1]), precision=HI)
    return jnp.sum(rows * low, axis=1)


def spread(values, high, low):
    return jnp.dot(high.T, values.reshape(-1)[:, None] * low, precision=HI).reshape(-1)


UNROLL = 64
ACCS = 8


def scatter_kernel(slots, pad, idx_ref, xs_ref, feat_ref, init_ref, out_ref, *accs):
    accs[0][...] = init_ref[...]
    for acc in accs[1:]:
        acc[...] = jnp.zeros(acc.shape, acc.dtype)

    def body(step, carry):
        row = step * UNROLL
        if pad:
            row = row + (row // slots) * pad
        for u in range(UNROLL):
            k = step * UNROLL + u
            acc = accs[u % ACCS]
            acc[pl.ds(idx_ref[k], 1), :] += xs_ref[k] * feat_ref[pl.ds(row + u, 1), :]
        return carry

    lax.fori_loop(0, idx_ref.shape[0] // UNROLL, body, 0)
    total = accs[0][...]
    for acc in accs[1:]:
        total = total + acc[...]
    out_ref[...] = total


def row_scatter(idx, xs, feat, init, slots=128, pad=0):
    smem = pl.BlockSpec(memory_space=pltpu.SMEM)
    vmem = pl.BlockSpec(memory_space=pltpu.VMEM)
    return pl.pallas_call(
        functools.partial(scatter_kernel, slots, pad),
        out_shape=jax.ShapeDtypeStruct(init.shape, jnp.float32),
        in_specs=[smem, smem, vmem, vmem],
        out_specs=vmem,
        scratch_shapes=[pltpu.VMEM(init.shape, jnp.float32) for _ in range(ACCS)],
    )(idx, xs, feat, init)


def gather_kernel(idx_ref, table_ref, feat_ref, out_ref, rows_ref):
    def body(step, carry):
        for u in range(UNROLL):
            k = step * UNROLL + u
            rows_ref[pl.ds(k, 1), :] = table_ref[pl.ds(idx_ref[k], 1), :]
        return carry

    lax.fori_loop(0, feat_ref.shape[0] // UNROLL, body, 0)
    lanes = feat_ref.shape[1]
    chunk = out_ref.shape[1]
    ones = jnp.ones((8, lanes), jnp.bfloat16)

    def reduce_chunk(c, carry):
        start = pl.multiple_of(c * chunk, chunk)
        prod = rows_ref[pl.ds(start, chunk), :] * feat_ref[pl.ds(start, chunk), :]
        sums = jnp.zeros((8, chunk), jnp.float32)
        for _ in range(3):
            part = prod.astype(jnp.bfloat16)
            prod = prod - part.astype(jnp.float32)
            sums = sums + lax.dot_general(
                ones, part, (((1,), (1,)), ((), ())), preferred_element_type=jnp.float32
            )
        out_ref[pl.ds(c, 1), :] = sums[0:1, :]
        return carry

    lax.fori_loop(0, out_ref.shape[0], reduce_chunk, 0)


def row_gather_dot(idx, table, feat):
    smem = pl.BlockSpec(memory_space=pltpu.SMEM)
    vmem = pl.BlockSpec(memory_space=pltpu.VMEM)
    return pl.pallas_call(
        gather_kernel,
        out_shape=jax.ShapeDtypeStruct((8, feat.shape[0] // 8), jnp.float32),
        in_specs=[smem, vmem, vmem],
        out_specs=vmem,
        scratch_shapes=[pltpu.VMEM(feat.shape, jnp.float32)],
    )(idx, table, feat)


def on_device(weights, seg_streamline, seg_features, pair_counts, seg_voxel, dictionary, measured):
    blocks = seg_streamline.shape[2]
    slots = seg_streamline.shape[3]
    coeffs = seg_features.shape[4]
    streams = weights.shape[0]
    stream_index = seg_streamline.reshape(blocks, slots)
    voxel_index = seg_voxel.reshape(blocks * slots)
    counts = pair_counts.reshape(blocks)
    live_slot = lax.broadcasted_iota(jnp.int32, (blocks, slots), 1) < counts[:, None]
    masked = jnp.where(
        live_slot[:, :, None], seg_features.reshape(blocks, slots, coeffs), jnp.float32(0.0)
    )
    high, low = one_hot_pair(stream_index, streams)
    half = slots // 2
    pad = 8
    picked = pick(weights, high, low).reshape(blocks, slots // coeffs, coeffs)
    first = jnp.concatenate(
        [masked[:, :half], picked, jnp.zeros((blocks, pad - slots // coeffs, coeffs), jnp.float32)],
        axis=1,
    )
    first = lax.all_to_all(first, "space", 0, 0, tiled=True)
    first, own_feat = lax.optimization_barrier((first, masked))
    column_sq = spread(jnp.sum(own_feat * own_feat, axis=2), high, low)
    scaling = 0.5 / (0.5 + column_sq)
    second = lax.all_to_all(masked[:, half:], "space", 0, 0, tiled=True)
    gram = lax.psum(jnp.dot(dictionary, dictionary.T, precision=HI), "shell")
    data_proj = lax.psum(jnp.dot(measured.T, dictionary.T, precision=HI), "shell")
    second, gram, data_proj = lax.optimization_barrier((second, gram, data_proj))
    first_x = first[:, half:half + slots // coeffs].reshape(blocks, slots)
    vox_parts = [voxel_index.reshape(blocks, slots)[:, h * half:(h + 1) * half].reshape(-1)
                 for h in range(2)]
    local_feat = jnp.concatenate([first[:, :half], second], axis=1).reshape(blocks * slots, coeffs)
    current = weights
    residual = jnp.zeros(measured.shape, jnp.float32)
    for iteration in range(ITERS):
        partial_coeff = jnp.zeros((measured.shape[1], coeffs), jnp.float32)
        if iteration == 0:
            partial_coeff = row_scatter(
                vox_parts[0], first_x[:, :half].reshape(-1),
                first.reshape(-1, coeffs), partial_coeff, half, pad,
            )
            partial_coeff = row_scatter(
                vox_parts[1], first_x[:, half:].reshape(-1),
                second.reshape(-1, coeffs), partial_coeff,
            )
        else:
            picked = pick(current, high, low).reshape(blocks, slots)
            local_x = lax.all_to_all(picked, "space", split_axis=0, concat_axis=0, tiled=True)
            partial_coeff = row_scatter(
                voxel_index, local_x.reshape(-1), local_feat, partial_coeff
            )
        coeff_sum = lax.psum(partial_coeff, "shell")
        if iteration == ITERS - 1:
            residual = (
                jnp.einsum("jg,vj->gv", dictionary, coeff_sum, precision=HI) - measured
            )
        adjoint = jnp.dot(coeff_sum, gram, precision=HI) - data_proj
        local_grad = row_gather_dot(voxel_index, adjoint, local_feat).reshape(blocks, slots)
        grad_slot = lax.all_to_all(local_grad, "space", split_axis=0, concat_axis=0, tiled=True)
        gradient = spread(grad_slot, high, low)
        current = jnp.maximum(current - scaling * gradient, 0.0)
    return (current, residual)


def solution(mesh):
    in_specs = (
        P(("space", "shell")),
        P("space", "shell", None, None),
        P("space", "shell", None, None, None),
        P("space", "shell", None),
        P("space", "shell", None, None),
        P(None, "shell"),
        P("shell", "space"),
    )
    out_specs = (P(("space", "shell")), P("shell", "space"))
    return jax.shard_map(
        on_device, mesh=mesh, in_specs=in_specs, out_specs=out_specs, check_vma=False
    )
```

```python
import functools

import jax
import jax.numpy as jnp
from jax import lax
from jax.sharding import PartitionSpec as P
from jax.experimental import pallas as pl
from jax.experimental.pallas import tpu as pltpu

ITERS = 2
HI = lax.Precision.HIGHEST


def one_hot_pair(index, count):
    low_count = 64
    high_count = count // low_count
    flat = index.reshape(-1)
    high = (flat // low_count)[:, None] == lax.broadcasted_iota(jnp.int32, (1, high_count), 1)
    low = (flat % low_count)[:, None] == lax.broadcasted_iota(jnp.int32, (1, low_count), 1)
    return high.astype(jnp.float32), low.astype(jnp.float32)


def pick(table, high, low):
    rows = jnp.dot(high, table.reshape(high.shape[1], low.shape[1]), precision=HI)
    return jnp.sum(rows * low, axis=1)


def spread(values, high, low):
    return jnp.dot(high.T, values.reshape(-1)[:, None] * low, precision=HI).reshape(-1)


UNROLL = 64
ACCS = 8


def scatter_kernel(slots, pad, idx_ref, xs_ref, feat_ref, init_ref, out_ref, *accs):
    accs[0][...] = init_ref[...]
    for acc in accs[1:]:
        acc[...] = jnp.zeros(acc.shape, acc.dtype)

    def body(step, carry):
        row = step * UNROLL
        if pad:
            row = row + (row // slots) * pad
        for u in range(UNROLL):
            k = step * UNROLL + u
            acc = accs[u % ACCS]
            acc[pl.ds(idx_ref[k], 1), :] += xs_ref[k] * feat_ref[pl.ds(row + u, 1), :]
        return carry

    lax.fori_loop(0, idx_ref.shape[0] // UNROLL, body, 0)
    total = accs[0][...]
    for acc in accs[1:]:
        total = total + acc[...]
    out_ref[...] = total


def row_scatter(idx, xs, feat, init, slots=128, pad=0):
    smem = pl.BlockSpec(memory_space=pltpu.SMEM)
    vmem = pl.BlockSpec(memory_space=pltpu.VMEM)
    return pl.pallas_call(
        functools.partial(scatter_kernel, slots, pad),
        out_shape=jax.ShapeDtypeStruct(init.shape, jnp.float32),
        in_specs=[smem, smem, vmem, vmem],
        out_specs=vmem,
        scratch_shapes=[pltpu.VMEM(init.shape, jnp.float32) for _ in range(ACCS)],
    )(idx, xs, feat, init)


def gather_kernel(idx_ref, table_ref, feat_ref, out_ref, rows_ref):
    def body(step, carry):
        for u in range(UNROLL):
            k = step * UNROLL + u
            rows_ref[pl.ds(k, 1), :] = table_ref[pl.ds(idx_ref[k], 1), :]
        return carry

    lax.fori_loop(0, feat_ref.shape[0] // UNROLL, body, 0)
    lanes = feat_ref.shape[1]
    chunk = out_ref.shape[1]
    ones = jnp.ones((8, lanes), jnp.bfloat16)

    def reduce_chunk(c, carry):
        start = pl.multiple_of(c * chunk, chunk)
        prod = rows_ref[pl.ds(start, chunk), :] * feat_ref[pl.ds(start, chunk), :]
        sums = jnp.zeros((8, chunk), jnp.float32)
        for _ in range(3):
            part = prod.astype(jnp.bfloat16)
            prod = prod - part.astype(jnp.float32)
            sums = sums + lax.dot_general(
                ones, part, (((1,), (1,)), ((), ())), preferred_element_type=jnp.float32
            )
        out_ref[pl.ds(c, 1), :] = sums[0:1, :]
        return carry

    lax.fori_loop(0, out_ref.shape[0], reduce_chunk, 0)


def row_gather_dot(idx, table, feat):
    smem = pl.BlockSpec(memory_space=pltpu.SMEM)
    vmem = pl.BlockSpec(memory_space=pltpu.VMEM)
    return pl.pallas_call(
        gather_kernel,
        out_shape=jax.ShapeDtypeStruct((8, feat.shape[0] // 8), jnp.float32),
        in_specs=[smem, vmem, vmem],
        out_specs=vmem,
        scratch_shapes=[pltpu.VMEM(feat.shape, jnp.float32)],
    )(idx, table, feat)


def on_device(weights, seg_streamline, seg_features, pair_counts, seg_voxel, dictionary, measured):
    blocks = seg_streamline.shape[2]
    slots = seg_streamline.shape[3]
    coeffs = seg_features.shape[4]
    streams = weights.shape[0]
    stream_index = seg_streamline.reshape(blocks, slots)
    voxel_index = seg_voxel.reshape(blocks * slots)
    counts = pair_counts.reshape(blocks)
    live_slot = lax.broadcasted_iota(jnp.int32, (blocks, slots), 1) < counts[:, None]
    raw = seg_features.reshape(blocks, slots, coeffs)
    high, low = one_hot_pair(stream_index, streams)
    half = slots // 2
    pad = 8
    x_rows = slots // coeffs
    picked = pick(weights, high, low).reshape(blocks, x_rows, coeffs)
    count_row = jnp.broadcast_to(counts.astype(jnp.float32)[:, None, None], (blocks, 1, coeffs))
    first = jnp.concatenate(
        [raw[:, :half], picked, count_row,
         jnp.zeros((blocks, pad - x_rows - 1, coeffs), jnp.float32)],
        axis=1,
    )
    first = lax.all_to_all(first, "space", 0, 0, tiled=True)
    first, own_feat = lax.optimization_barrier((first, raw))
    masked_sq = jnp.where(live_slot, jnp.sum(own_feat * own_feat, axis=2), jnp.float32(0.0))
    column_sq = spread(masked_sq, high, low)
    scaling = 0.5 / (0.5 + column_sq)
    second = lax.all_to_all(raw[:, half:], "space", 0, 0, tiled=True)
    gram = lax.psum(jnp.dot(dictionary, dictionary.T, precision=HI), "shell")
    data_proj = lax.psum(jnp.dot(measured.T, dictionary.T, precision=HI), "shell")
    second, gram, data_proj = lax.optimization_barrier((second, gram, data_proj))
    source_count = first[:, half + x_rows, 0]
    live_here = (
        lax.broadcasted_iota(jnp.int32, (blocks, slots), 1).astype(jnp.float32)
        < source_count[:, None]
    )
    first_x = jnp.where(live_here, first[:, half:half + x_rows].reshape(blocks, slots), 0.0)
    vox_parts = [voxel_index.reshape(blocks, slots)[:, h * half:(h + 1) * half].reshape(-1)
                 for h in range(2)]
    local_feat = jnp.concatenate([first[:, :half], second], axis=1).reshape(blocks * slots, coeffs)
    current = weights
    residual = jnp.zeros(measured.shape, jnp.float32)
    for iteration in range(ITERS):
        partial_coeff = jnp.zeros((measured.shape[1], coeffs), jnp.float32)
        if iteration == 0:
            partial_coeff = row_scatter(
                vox_parts[0], first_x[:, :half].reshape(-1),
                first.reshape(-1, coeffs), partial_coeff, half, pad,
            )
            partial_coeff = row_scatter(
                vox_parts[1], first_x[:, half:].reshape(-1),
                second.reshape(-1, coeffs), partial_coeff,
            )
        else:
            picked = pick(current, high, low).reshape(blocks, slots)
            local_x = lax.all_to_all(picked, "space", split_axis=0, concat_axis=0, tiled=True)
            local_x = jnp.where(live_here, local_x, 0.0)
            partial_coeff = row_scatter(
                voxel_index, local_x.reshape(-1), local_feat, partial_coeff
            )
        coeff_sum = lax.psum(partial_coeff, "shell")
        if iteration == ITERS - 1:
            residual = (
                jnp.einsum("jg,vj->gv", dictionary, coeff_sum, precision=HI) - measured
            )
        adjoint = jnp.dot(coeff_sum, gram, precision=HI) - data_proj
        local_grad = row_gather_dot(voxel_index, adjoint, local_feat).reshape(blocks, slots)
        local_grad = jnp.where(live_here, local_grad, 0.0)
        grad_slot = lax.all_to_all(local_grad, "space", split_axis=0, concat_axis=0, tiled=True)
        gradient = spread(grad_slot, high, low)
        current = jnp.maximum(current - scaling * gradient, 0.0)
    return (current, residual)


def solution(mesh):
    in_specs = (
        P(("space", "shell")),
        P("space", "shell", None, None),
        P("space", "shell", None, None, None),
        P("space", "shell", None),
        P("space", "shell", None, None),
        P(None, "shell"),
        P("shell", "space"),
    )
    out_specs = (P(("space", "shell")), P("shell", "space"))
    return jax.shard_map(
        on_device, mesh=mesh, in_specs=in_specs, out_specs=out_specs, check_vma=False
    )
```

```python
import functools

import jax
import jax.numpy as jnp
from jax import lax
from jax.sharding import PartitionSpec as P
from jax.experimental import pallas as pl
from jax.experimental.pallas import tpu as pltpu

ITERS = 2
HI = lax.Precision.HIGHEST


def one_hot_pair(index, count):
    low_count = 64
    high_count = count // low_count
    flat = index.reshape(-1)
    high = (flat // low_count)[:, None] == lax.broadcasted_iota(jnp.int32, (1, high_count), 1)
    low = (flat % low_count)[:, None] == lax.broadcasted_iota(jnp.int32, (1, low_count), 1)
    return high.astype(jnp.float32), low.astype(jnp.float32)


def pick(table, high, low):
    rows = jnp.dot(high, table.reshape(high.shape[1], low.shape[1]), precision=HI)
    return jnp.sum(rows * low, axis=1)


def spread(values, high, low):
    return jnp.dot(high.T, values.reshape(-1)[:, None] * low, precision=HI).reshape(-1)


UNROLL = 64
ACCS = 8


def scatter_kernel(slots, pad, idx_ref, xs_ref, feat_ref, init_ref, out_ref, *accs):
    accs[0][...] = init_ref[...]
    for acc in accs[1:]:
        acc[...] = jnp.zeros(acc.shape, acc.dtype)

    def body(step, carry):
        row = step * UNROLL
        if pad:
            row = row + (row // slots) * pad
        for u in range(UNROLL):
            k = step * UNROLL + u
            acc = accs[u % ACCS]
            acc[pl.ds(idx_ref[k], 1), :] += xs_ref[k] * feat_ref[pl.ds(row + u, 1), :]
        return carry

    lax.fori_loop(0, idx_ref.shape[0] // UNROLL, body, 0)
    total = accs[0][...]
    for acc in accs[1:]:
        total = total + acc[...]
    out_ref[...] = total


def row_scatter(idx, xs, feat, init, slots=128, pad=0):
    smem = pl.BlockSpec(memory_space=pltpu.SMEM)
    vmem = pl.BlockSpec(memory_space=pltpu.VMEM)
    return pl.pallas_call(
        functools.partial(scatter_kernel, slots, pad),
        out_shape=jax.ShapeDtypeStruct(init.shape, jnp.float32),
        in_specs=[smem, smem, vmem, vmem],
        out_specs=vmem,
        scratch_shapes=[pltpu.VMEM(init.shape, jnp.float32) for _ in range(ACCS)],
    )(idx, xs, feat, init)


def gather_kernel(idx_ref, table_ref, feat_ref, out_ref, rows_ref):
    def body(step, carry):
        for u in range(UNROLL):
            k = step * UNROLL + u
            rows_ref[pl.ds(k, 1), :] = table_ref[pl.ds(idx_ref[k], 1), :]
        return carry

    lax.fori_loop(0, feat_ref.shape[0] // UNROLL, body, 0)
    lanes = feat_ref.shape[1]
    chunk = out_ref.shape[1]
    ones = jnp.ones((8, lanes), jnp.bfloat16)

    def reduce_chunk(c, carry):
        start = pl.multiple_of(c * chunk, chunk)
        prod = rows_ref[pl.ds(start, chunk), :] * feat_ref[pl.ds(start, chunk), :]
        sums = jnp.zeros((8, chunk), jnp.float32)
        for _ in range(3):
            part = prod.astype(jnp.bfloat16)
            prod = prod - part.astype(jnp.float32)
            sums = sums + lax.dot_general(
                ones, part, (((1,), (1,)), ((), ())), preferred_element_type=jnp.float32
            )
        out_ref[pl.ds(c, 1), :] = sums[0:1, :]
        return carry

    lax.fori_loop(0, out_ref.shape[0], reduce_chunk, 0)


def row_gather_dot(idx, table, feat):
    smem = pl.BlockSpec(memory_space=pltpu.SMEM)
    vmem = pl.BlockSpec(memory_space=pltpu.VMEM)
    return pl.pallas_call(
        gather_kernel,
        out_shape=jax.ShapeDtypeStruct((8, feat.shape[0] // 8), jnp.float32),
        in_specs=[smem, vmem, vmem],
        out_specs=vmem,
        scratch_shapes=[pltpu.VMEM(feat.shape, jnp.float32)],
    )(idx, table, feat)


def on_device(weights, seg_streamline, seg_features, pair_counts, seg_voxel, dictionary, measured):
    blocks = seg_streamline.shape[2]
    slots = seg_streamline.shape[3]
    coeffs = seg_features.shape[4]
    streams = weights.shape[0]
    stream_index = seg_streamline.reshape(blocks, slots)
    voxel_index = seg_voxel.reshape(blocks * slots)
    counts = pair_counts.reshape(blocks)
    live_slot = lax.broadcasted_iota(jnp.int32, (blocks, slots), 1) < counts[:, None]
    raw = seg_features.reshape(blocks, slots, coeffs)
    high, low = one_hot_pair(stream_index, streams)
    half = slots // 2
    pad = 8
    x_rows = slots // coeffs
    picked = pick(weights, high, low).reshape(blocks, x_rows, coeffs)
    count_row = jnp.broadcast_to(counts.astype(jnp.float32)[:, None, None], (blocks, 1, coeffs))
    first = jnp.concatenate(
        [raw[:, :half], picked, count_row,
         jnp.zeros((blocks, pad - x_rows - 1, coeffs), jnp.float32)],
        axis=1,
    )
    first = lax.all_to_all(first, "space", 0, 0, tiled=True)
    first, own_feat = lax.optimization_barrier((first, raw))
    masked_sq = jnp.where(live_slot, jnp.sum(own_feat * own_feat, axis=2), jnp.float32(0.0))
    column_sq = spread(masked_sq, high, low)
    scaling = 0.5 / (0.5 + column_sq)
    second = lax.all_to_all(own_feat[:, half:], "space", 0, 0, tiled=True)
    gram = lax.psum(jnp.dot(dictionary, dictionary.T, precision=HI), "shell")
    data_proj = lax.psum(jnp.dot(measured.T, dictionary.T, precision=HI), "shell")
    second, gram, data_proj = lax.optimization_barrier((second, gram, data_proj))
    source_count = first[:, half + x_rows, 0]
    live_here = (
        lax.broadcasted_iota(jnp.int32, (blocks, slots), 1).astype(jnp.float32)
        < source_count[:, None]
    )
    first_x = jnp.where(live_here, first[:, half:half + x_rows].reshape(blocks, slots), 0.0)
    vox_parts = [voxel_index.reshape(blocks, slots)[:, h * half:(h + 1) * half].reshape(-1)
                 for h in range(2)]
    local_feat = jnp.concatenate([first[:, :half], second], axis=1).reshape(blocks * slots, coeffs)
    current = weights
    residual = jnp.zeros(measured.shape, jnp.float32)
    for iteration in range(ITERS):
        partial_coeff = jnp.zeros((measured.shape[1], coeffs), jnp.float32)
        if iteration == 0:
            partial_coeff = row_scatter(
                vox_parts[0], first_x[:, :half].reshape(-1),
                first.reshape(-1, coeffs), partial_coeff, half, pad,
            )
            partial_coeff = row_scatter(
                vox_parts[1], first_x[:, half:].reshape(-1),
                second.reshape(-1, coeffs), partial_coeff,
            )
        else:
            picked = pick(current, high, low).reshape(blocks, slots)
            local_x = lax.all_to_all(picked, "space", split_axis=0, concat_axis=0, tiled=True)
            local_x = jnp.where(live_here, local_x, 0.0)
            partial_coeff = row_scatter(
                voxel_index, local_x.reshape(-1), local_feat, partial_coeff
            )
        coeff_sum = lax.psum(partial_coeff, "shell")
        if iteration == ITERS - 1:
            residual = (
                jnp.einsum("jg,vj->gv", dictionary, coeff_sum, precision=HI) - measured
            )
        adjoint = jnp.dot(coeff_sum, gram, precision=HI) - data_proj
        local_grad = row_gather_dot(voxel_index, adjoint, local_feat).reshape(blocks, slots)
        local_grad = jnp.where(live_here, local_grad, 0.0)
        grad_slot = lax.all_to_all(local_grad, "space", split_axis=0, concat_axis=0, tiled=True)
        gradient = spread(grad_slot, high, low)
        current = jnp.maximum(current - scaling * gradient, 0.0)
    return (current, residual)


def solution(mesh):
    in_specs = (
        P(("space", "shell")),
        P("space", "shell", None, None),
        P("space", "shell", None, None, None),
        P("space", "shell", None),
        P("space", "shell", None, None),
        P(None, "shell"),
        P("shell", "space"),
    )
    out_specs = (P(("space", "shell")), P("shell", "space"))
    return jax.shard_map(
        on_device, mesh=mesh, in_specs=in_specs, out_specs=out_specs, check_vma=False
    )
```

```python
import functools

import jax
import jax.numpy as jnp
from jax import lax
from jax.sharding import PartitionSpec as P
from jax.experimental import pallas as pl
from jax.experimental.pallas import tpu as pltpu

ITERS = 2
HI = lax.Precision.HIGHEST


def one_hot_pair(index, count):
    low_count = 64
    high_count = count // low_count
    flat = index.reshape(-1)
    high = (flat // low_count)[:, None] == lax.broadcasted_iota(jnp.int32, (1, high_count), 1)
    low = (flat % low_count)[:, None] == lax.broadcasted_iota(jnp.int32, (1, low_count), 1)
    return high.astype(jnp.float32), low.astype(jnp.float32)


def pick(table, high, low):
    rows = jnp.dot(high, table.reshape(high.shape[1], low.shape[1]), precision=HI)
    return jnp.sum(rows * low, axis=1)


def spread(values, high, low):
    return jnp.dot(high.T, values.reshape(-1)[:, None] * low, precision=HI).reshape(-1)


UNROLL = 64
ACCS = 8


def scatter_kernel(slots, pad, idx_ref, xs_ref, feat_ref, init_ref, out_ref, *accs):
    accs[0][...] = init_ref[...]
    for acc in accs[1:]:
        acc[...] = jnp.zeros(acc.shape, acc.dtype)

    def body(step, carry):
        row = step * UNROLL
        if pad:
            row = row + (row // slots) * pad
        for u in range(UNROLL):
            k = step * UNROLL + u
            acc = accs[u % ACCS]
            acc[pl.ds(idx_ref[k], 1), :] += xs_ref[k] * feat_ref[pl.ds(row + u, 1), :]
        return carry

    lax.fori_loop(0, idx_ref.shape[0] // UNROLL, body, 0)
    total = accs[0][...]
    for acc in accs[1:]:
        total = total + acc[...]
    out_ref[...] = total


def row_scatter(idx, xs, feat, init, slots=128, pad=0):
    smem = pl.BlockSpec(memory_space=pltpu.SMEM)
    vmem = pl.BlockSpec(memory_space=pltpu.VMEM)
    return pl.pallas_call(
        functools.partial(scatter_kernel, slots, pad),
        out_shape=jax.ShapeDtypeStruct(init.shape, jnp.float32),
        in_specs=[smem, smem, vmem, vmem],
        out_specs=vmem,
        scratch_shapes=[pltpu.VMEM(init.shape, jnp.float32) for _ in range(ACCS)],
    )(idx, xs, feat, init)


def gather_kernel(idx_ref, table_ref, feat_ref, out_ref, rows_ref):
    def body(step, carry):
        for u in range(UNROLL):
            k = step * UNROLL + u
            rows_ref[pl.ds(k, 1), :] = table_ref[pl.ds(idx_ref[k], 1), :]
        return carry

    lax.fori_loop(0, feat_ref.shape[0] // UNROLL, body, 0)
    lanes = feat_ref.shape[1]
    chunk = out_ref.shape[1]
    ones = jnp.ones((8, lanes), jnp.bfloat16)

    def reduce_chunk(c, carry):
        start = pl.multiple_of(c * chunk, chunk)
        prod = rows_ref[pl.ds(start, chunk), :] * feat_ref[pl.ds(start, chunk), :]
        sums = jnp.zeros((8, chunk), jnp.float32)
        for _ in range(3):
            part = prod.astype(jnp.bfloat16)
            prod = prod - part.astype(jnp.float32)
            sums = sums + lax.dot_general(
                ones, part, (((1,), (1,)), ((), ())), preferred_element_type=jnp.float32
            )
        out_ref[pl.ds(c, 1), :] = sums[0:1, :]
        return carry

    lax.fori_loop(0, out_ref.shape[0], reduce_chunk, 0)


def row_gather_dot(idx, table, feat):
    smem = pl.BlockSpec(memory_space=pltpu.SMEM)
    vmem = pl.BlockSpec(memory_space=pltpu.VMEM)
    return pl.pallas_call(
        gather_kernel,
        out_shape=jax.ShapeDtypeStruct((8, feat.shape[0] // 8), jnp.float32),
        in_specs=[smem, vmem, vmem],
        out_specs=vmem,
        scratch_shapes=[pltpu.VMEM(feat.shape, jnp.float32)],
    )(idx, table, feat)


def on_device(weights, seg_streamline, seg_features, pair_counts, seg_voxel, dictionary, measured):
    blocks = seg_streamline.shape[2]
    slots = seg_streamline.shape[3]
    coeffs = seg_features.shape[4]
    streams = weights.shape[0]
    stream_index = seg_streamline.reshape(blocks, slots)
    voxel_index = seg_voxel.reshape(blocks * slots)
    counts = pair_counts.reshape(blocks)
    live_slot = lax.broadcasted_iota(jnp.int32, (blocks, slots), 1) < counts[:, None]
    raw = seg_features.reshape(blocks, slots, coeffs)
    high, low = one_hot_pair(stream_index, streams)
    half = slots // 2
    pad = 8
    x_rows = slots // coeffs
    picked = pick(weights, high, low).reshape(blocks, x_rows, coeffs)
    count_row = jnp.broadcast_to(counts.astype(jnp.float32)[:, None, None], (blocks, 1, coeffs))
    first = jnp.concatenate(
        [raw[:, :half], picked, count_row,
         jnp.zeros((blocks, pad - x_rows - 1, coeffs), jnp.float32)],
        axis=1,
    )
    first = lax.all_to_all(first, "space", 0, 0, tiled=True)
    first, own_feat = lax.optimization_barrier((first, raw))
    masked_sq = jnp.where(live_slot, jnp.sum(own_feat * own_feat, axis=2), jnp.float32(0.0))
    column_sq = spread(masked_sq, high, low)
    scaling = 0.5 / (0.5 + column_sq)
    shell_proj = jnp.dot(measured.T, dictionary.T, precision=HI)
    shell_proj, later_feat = lax.optimization_barrier((shell_proj, raw))
    second = lax.all_to_all(later_feat[:, half:], "space", 0, 0, tiled=True)
    gram = lax.psum(jnp.dot(dictionary, dictionary.T, precision=HI), "shell")
    data_proj = lax.psum(shell_proj, "shell")
    second, gram, data_proj = lax.optimization_barrier((second, gram, data_proj))
    source_count = first[:, half + x_rows, 0]
    live_here = (
        lax.broadcasted_iota(jnp.int32, (blocks, slots), 1).astype(jnp.float32)
        < source_count[:, None]
    )
    first_x = jnp.where(live_here, first[:, half:half + x_rows].reshape(blocks, slots), 0.0)
    vox_parts = [voxel_index.reshape(blocks, slots)[:, h * half:(h + 1) * half].reshape(-1)
                 for h in range(2)]
    local_feat = jnp.concatenate([first[:, :half], second], axis=1).reshape(blocks * slots, coeffs)
    current = weights
    residual = jnp.zeros(measured.shape, jnp.float32)
    for iteration in range(ITERS):
        partial_coeff = jnp.zeros((measured.shape[1], coeffs), jnp.float32)
        if iteration == 0:
            partial_coeff = row_scatter(
                vox_parts[0], first_x[:, :half].reshape(-1),
                first.reshape(-1, coeffs), partial_coeff, half, pad,
            )
            partial_coeff = row_scatter(
                vox_parts[1], first_x[:, half:].reshape(-1),
                second.reshape(-1, coeffs), partial_coeff,
            )
        else:
            picked = pick(current, high, low).reshape(blocks, slots)
            local_x = lax.all_to_all(picked, "space", split_axis=0, concat_axis=0, tiled=True)
            local_x = jnp.where(live_here, local_x, 0.0)
            partial_coeff = row_scatter(
                voxel_index, local_x.reshape(-1), local_feat, partial_coeff
            )
        coeff_sum = lax.psum(partial_coeff, "shell")
        if iteration == ITERS - 1:
            residual = (
                jnp.einsum("jg,vj->gv", dictionary, coeff_sum, precision=HI) - measured
            )
        adjoint = jnp.dot(coeff_sum, gram, precision=HI) - data_proj
        local_grad = row_gather_dot(voxel_index, adjoint, local_feat).reshape(blocks, slots)
        local_grad = jnp.where(live_here, local_grad, 0.0)
        grad_slot = lax.all_to_all(local_grad, "space", split_axis=0, concat_axis=0, tiled=True)
        gradient = spread(grad_slot, high, low)
        current = jnp.maximum(current - scaling * gradient, 0.0)
    return (current, residual)


def solution(mesh):
    in_specs = (
        P(("space", "shell")),
        P("space", "shell", None, None),
        P("space", "shell", None, None, None),
        P("space", "shell", None),
        P("space", "shell", None, None),
        P(None, "shell"),
        P("shell", "space"),
    )
    out_specs = (P(("space", "shell")), P("shell", "space"))
    return jax.shard_map(
        on_device, mesh=mesh, in_specs=in_specs, out_specs=out_specs, check_vma=False
    )
```

```python
import functools

import jax
import jax.numpy as jnp
from jax import lax
from jax.sharding import PartitionSpec as P
from jax.experimental import pallas as pl
from jax.experimental.pallas import tpu as pltpu

ITERS = 2
HI = lax.Precision.HIGHEST


def one_hot_pair(index, count):
    low_count = 64
    high_count = count // low_count
    flat = index.reshape(-1)
    high = (flat // low_count)[:, None] == lax.broadcasted_iota(jnp.int32, (1, high_count), 1)
    low = (flat % low_count)[:, None] == lax.broadcasted_iota(jnp.int32, (1, low_count), 1)
    return high.astype(jnp.float32), low.astype(jnp.float32)


def pick(table, high, low):
    rows = jnp.dot(high, table.reshape(high.shape[1], low.shape[1]), precision=HI)
    return jnp.sum(rows * low, axis=1)


def spread(values, high, low):
    return jnp.dot(high.T, values.reshape(-1)[:, None] * low, precision=HI).reshape(-1)


UNROLL = 64
ACCS = 8


def scatter_kernel(slots, pad, has_init, idx_ref, xs_ref, feat_ref, *refs):
    if has_init:
        init_ref, out_ref, *accs = refs
        accs[0][...] = init_ref[...]
    else:
        out_ref, *accs = refs
        accs[0][...] = jnp.zeros(accs[0].shape, accs[0].dtype)
    for acc in accs[1:]:
        acc[...] = jnp.zeros(acc.shape, acc.dtype)

    def body(step, carry):
        row = step * UNROLL
        if pad:
            row = row + (row // slots) * pad
        for u in range(UNROLL):
            k = step * UNROLL + u
            acc = accs[u % ACCS]
            acc[pl.ds(idx_ref[k], 1), :] += xs_ref[k] * feat_ref[pl.ds(row + u, 1), :]
        return carry

    lax.fori_loop(0, idx_ref.shape[0] // UNROLL, body, 0)
    total = accs[0][...]
    for acc in accs[1:]:
        total = total + acc[...]
    out_ref[...] = total


def row_scatter(idx, xs, feat, init, slots=128, pad=0, rows=None):
    smem = pl.BlockSpec(memory_space=pltpu.SMEM)
    vmem = pl.BlockSpec(memory_space=pltpu.VMEM)
    shape = init.shape if init is not None else (rows, feat.shape[1])
    operands = (idx, xs, feat) if init is None else (idx, xs, feat, init)
    return pl.pallas_call(
        functools.partial(scatter_kernel, slots, pad, init is not None),
        out_shape=jax.ShapeDtypeStruct(shape, jnp.float32),
        in_specs=[smem, smem] + [vmem] * (len(operands) - 2),
        out_specs=vmem,
        scratch_shapes=[pltpu.VMEM(shape, jnp.float32) for _ in range(ACCS)],
    )(*operands)


def gather_kernel(idx_ref, table_ref, feat_ref, out_ref, rows_ref):
    def body(step, carry):
        for u in range(UNROLL):
            k = step * UNROLL + u
            rows_ref[pl.ds(k, 1), :] = table_ref[pl.ds(idx_ref[k], 1), :]
        return carry

    lax.fori_loop(0, feat_ref.shape[0] // UNROLL, body, 0)
    lanes = feat_ref.shape[1]
    chunk = out_ref.shape[1]
    ones = jnp.ones((8, lanes), jnp.bfloat16)

    def reduce_chunk(c, carry):
        start = pl.multiple_of(c * chunk, chunk)
        prod = rows_ref[pl.ds(start, chunk), :] * feat_ref[pl.ds(start, chunk), :]
        sums = jnp.zeros((8, chunk), jnp.float32)
        for _ in range(3):
            part = prod.astype(jnp.bfloat16)
            prod = prod - part.astype(jnp.float32)
            sums = sums + lax.dot_general(
                ones, part, (((1,), (1,)), ((), ())), preferred_element_type=jnp.float32
            )
        out_ref[pl.ds(c, 1), :] = sums[0:1, :]
        return carry

    lax.fori_loop(0, out_ref.shape[0], reduce_chunk, 0)


def row_gather_dot(idx, table, feat):
    smem = pl.BlockSpec(memory_space=pltpu.SMEM)
    vmem = pl.BlockSpec(memory_space=pltpu.VMEM)
    return pl.pallas_call(
        gather_kernel,
        out_shape=jax.ShapeDtypeStruct((8, feat.shape[0] // 8), jnp.float32),
        in_specs=[smem, vmem, vmem],
        out_specs=vmem,
        scratch_shapes=[pltpu.VMEM(feat.shape, jnp.float32)],
    )(idx, table, feat)


def on_device(weights, seg_streamline, seg_features, pair_counts, seg_voxel, dictionary, measured):
    blocks = seg_streamline.shape[2]
    slots = seg_streamline.shape[3]
    coeffs = seg_features.shape[4]
    streams = weights.shape[0]
    stream_index = seg_streamline.reshape(blocks, slots)
    voxel_index = seg_voxel.reshape(blocks * slots)
    counts = pair_counts.reshape(blocks)
    live_slot = lax.broadcasted_iota(jnp.int32, (blocks, slots), 1) < counts[:, None]
    raw = seg_features.reshape(blocks, slots, coeffs)
    high, low = one_hot_pair(stream_index, streams)
    half = slots // 2
    pad = 8
    x_rows = slots // coeffs
    picked = pick(weights, high, low).reshape(blocks, x_rows, coeffs)
    count_row = jnp.broadcast_to(counts.astype(jnp.float32)[:, None, None], (blocks, 1, coeffs))
    first = jnp.concatenate(
        [raw[:, :half], picked, count_row,
         jnp.zeros((blocks, pad - x_rows - 1, coeffs), jnp.float32)],
        axis=1,
    )
    first = lax.all_to_all(first, "space", 0, 0, tiled=True)
    first, own_feat = lax.optimization_barrier((first, raw))
    masked_sq = jnp.where(live_slot, jnp.sum(own_feat * own_feat, axis=2), jnp.float32(0.0))
    column_sq = spread(masked_sq, high, low)
    scaling = 0.5 / (0.5 + column_sq)
    second = lax.all_to_all(own_feat[:, half:], "space", 0, 0, tiled=True)
    gram = lax.psum(jnp.dot(dictionary, dictionary.T, precision=HI), "shell")
    data_proj = lax.psum(jnp.dot(measured.T, dictionary.T, precision=HI), "shell")
    second, gram, data_proj = lax.optimization_barrier((second, gram, data_proj))
    source_count = first[:, half + x_rows, 0]
    live_here = (
        lax.broadcasted_iota(jnp.int32, (blocks, slots), 1).astype(jnp.float32)
        < source_count[:, None]
    )
    first_x = jnp.where(live_here, first[:, half:half + x_rows].reshape(blocks, slots), 0.0)
    vox_parts = [voxel_index.reshape(blocks, slots)[:, h * half:(h + 1) * half].reshape(-1)
                 for h in range(2)]
    local_feat = jnp.concatenate([first[:, :half], second], axis=1).reshape(blocks * slots, coeffs)
    current = weights
    residual = jnp.zeros(measured.shape, jnp.float32)
    for iteration in range(ITERS):
        if iteration == 0:
            partial_coeff = row_scatter(
                vox_parts[0], first_x[:, :half].reshape(-1),
                first.reshape(-1, coeffs), None, half, pad, measured.shape[1],
            )
            partial_coeff = row_scatter(
                vox_parts[1], first_x[:, half:].reshape(-1),
                second.reshape(-1, coeffs), partial_coeff,
            )
        else:
            picked = pick(current, high, low).reshape(blocks, slots)
            local_x = lax.all_to_all(picked, "space", split_axis=0, concat_axis=0, tiled=True)
            local_x = jnp.where(live_here, local_x, 0.0)
            partial_coeff = row_scatter(
                voxel_index, local_x.reshape(-1), local_feat, None, rows=measured.shape[1]
            )
        coeff_sum = lax.psum(partial_coeff, "shell")
        if iteration == ITERS - 1:
            residual = (
                jnp.einsum("jg,vj->gv", dictionary, coeff_sum, precision=HI) - measured
            )
        adjoint = jnp.dot(coeff_sum, gram, precision=HI) - data_proj
        local_grad = row_gather_dot(voxel_index, adjoint, local_feat).reshape(blocks, slots)
        local_grad = jnp.where(live_here, local_grad, 0.0)
        grad_slot = lax.all_to_all(local_grad, "space", split_axis=0, concat_axis=0, tiled=True)
        gradient = spread(grad_slot, high, low)
        current = jnp.maximum(current - scaling * gradient, 0.0)
    return (current, residual)


def solution(mesh):
    in_specs = (
        P(("space", "shell")),
        P("space", "shell", None, None),
        P("space", "shell", None, None, None),
        P("space", "shell", None),
        P("space", "shell", None, None),
        P(None, "shell"),
        P("shell", "space"),
    )
    out_specs = (P(("space", "shell")), P("shell", "space"))
    return jax.shard_map(
        on_device, mesh=mesh, in_specs=in_specs, out_specs=out_specs, check_vma=False
    )
```

```python
import functools

import jax
import jax.numpy as jnp
from jax import lax
from jax.sharding import PartitionSpec as P
from jax.experimental import pallas as pl
from jax.experimental.pallas import tpu as pltpu

ITERS = 2
HI = lax.Precision.HIGHEST


def one_hot_pair(index, count):
    low_count = 64
    high_count = count // low_count
    flat = index.reshape(-1)
    high = (flat // low_count)[:, None] == lax.broadcasted_iota(jnp.int32, (1, high_count), 1)
    low = (flat % low_count)[:, None] == lax.broadcasted_iota(jnp.int32, (1, low_count), 1)
    return high.astype(jnp.float32), low.astype(jnp.float32)


def pick(table, high, low):
    rows = jnp.dot(high, table.reshape(high.shape[1], low.shape[1]), precision=HI)
    return jnp.sum(rows * low, axis=1)


def spread(values, high, low):
    return jnp.dot(high.T, values.reshape(-1)[:, None] * low, precision=HI).reshape(-1)


UNROLL = 64
ACCS = 8


def scatter_kernel(slots, pad, idx_ref, xs_ref, feat_ref, init_ref, out_ref, *accs):
    accs[0][...] = init_ref[...]
    for acc in accs[1:]:
        acc[...] = jnp.zeros(acc.shape, acc.dtype)

    def body(step, carry):
        row = step * UNROLL
        if pad:
            row = row + (row // slots) * pad
        for u in range(UNROLL):
            k = step * UNROLL + u
            acc = accs[u % ACCS]
            acc[pl.ds(idx_ref[k], 1), :] += xs_ref[k] * feat_ref[pl.ds(row + u, 1), :]
        return carry

    lax.fori_loop(0, idx_ref.shape[0] // UNROLL, body, 0)
    total = accs[0][...]
    for acc in accs[1:]:
        total = total + acc[...]
    out_ref[...] = total


def row_scatter(idx, xs, feat, init, slots=128, pad=0):
    smem = pl.BlockSpec(memory_space=pltpu.SMEM)
    vmem = pl.BlockSpec(memory_space=pltpu.VMEM)
    return pl.pallas_call(
        functools.partial(scatter_kernel, slots, pad),
        out_shape=jax.ShapeDtypeStruct(init.shape, jnp.float32),
        in_specs=[smem, smem, vmem, vmem],
        out_specs=vmem,
        scratch_shapes=[pltpu.VMEM(init.shape, jnp.float32) for _ in range(ACCS)],
    )(idx, xs, feat, init)


def gather_kernel(idx_ref, table_ref, feat_ref, out_ref, rows_ref):
    def body(step, carry):
        for u in range(2 * UNROLL):
            k = step * 2 * UNROLL + u
            rows_ref[pl.ds(k, 1), :] = table_ref[pl.ds(idx_ref[k], 1), :]
        return carry

    lax.fori_loop(0, feat_ref.shape[0] // (2 * UNROLL), body, 0)
    lanes = feat_ref.shape[1]
    chunk = out_ref.shape[1]
    ones = jnp.ones((8, lanes), jnp.bfloat16)

    def reduce_chunk(c, carry):
        start = pl.multiple_of(c * chunk, chunk)
        prod = rows_ref[pl.ds(start, chunk), :] * feat_ref[pl.ds(start, chunk), :]
        sums = jnp.zeros((8, chunk), jnp.float32)
        for _ in range(3):
            part = prod.astype(jnp.bfloat16)
            prod = prod - part.astype(jnp.float32)
            sums = sums + lax.dot_general(
                ones, part, (((1,), (1,)), ((), ())), preferred_element_type=jnp.float32
            )
        out_ref[pl.ds(c, 1), :] = sums[0:1, :]
        return carry

    lax.fori_loop(0, out_ref.shape[0], reduce_chunk, 0)


def row_gather_dot(idx, table, feat):
    smem = pl.BlockSpec(memory_space=pltpu.SMEM)
    vmem = pl.BlockSpec(memory_space=pltpu.VMEM)
    return pl.pallas_call(
        gather_kernel,
        out_shape=jax.ShapeDtypeStruct((8, feat.shape[0] // 8), jnp.float32),
        in_specs=[smem, vmem, vmem],
        out_specs=vmem,
        scratch_shapes=[pltpu.VMEM(feat.shape, jnp.float32)],
    )(idx, table, feat)


def on_device(weights, seg_streamline, seg_features, pair_counts, seg_voxel, dictionary, measured):
    blocks = seg_streamline.shape[2]
    slots = seg_streamline.shape[3]
    coeffs = seg_features.shape[4]
    streams = weights.shape[0]
    stream_index = seg_streamline.reshape(blocks, slots)
    voxel_index = seg_voxel.reshape(blocks * slots)
    counts = pair_counts.reshape(blocks)
    live_slot = lax.broadcasted_iota(jnp.int32, (blocks, slots), 1) < counts[:, None]
    raw = seg_features.reshape(blocks, slots, coeffs)
    high, low = one_hot_pair(stream_index, streams)
    half = slots // 2
    pad = 8
    x_rows = slots // coeffs
    picked = pick(weights, high, low).reshape(blocks, x_rows, coeffs)
    count_row = jnp.broadcast_to(counts.astype(jnp.float32)[:, None, None], (blocks, 1, coeffs))
    first = jnp.concatenate(
        [raw[:, :half], picked, count_row,
         jnp.zeros((blocks, pad - x_rows - 1, coeffs), jnp.float32)],
        axis=1,
    )
    first = lax.all_to_all(first, "space", 0, 0, tiled=True)
    first, own_feat = lax.optimization_barrier((first, raw))
    masked_sq = jnp.where(live_slot, jnp.sum(own_feat * own_feat, axis=2), jnp.float32(0.0))
    column_sq = spread(masked_sq, high, low)
    scaling = 0.5 / (0.5 + column_sq)
    second = lax.all_to_all(own_feat[:, half:], "space", 0, 0, tiled=True)
    gram = lax.psum(jnp.dot(dictionary, dictionary.T, precision=HI), "shell")
    data_proj = lax.psum(jnp.dot(measured.T, dictionary.T, precision=HI), "shell")
    second, gram, data_proj = lax.optimization_barrier((second, gram, data_proj))
    source_count = first[:, half + x_rows, 0]
    live_here = (
        lax.broadcasted_iota(jnp.int32, (blocks, slots), 1).astype(jnp.float32)
        < source_count[:, None]
    )
    first_x = jnp.where(live_here, first[:, half:half + x_rows].reshape(blocks, slots), 0.0)
    vox_parts = [voxel_index.reshape(blocks, slots)[:, h * half:(h + 1) * half].reshape(-1)
                 for h in range(2)]
    local_feat = jnp.concatenate([first[:, :half], second], axis=1).reshape(blocks * slots, coeffs)
    current = weights
    residual = jnp.zeros(measured.shape, jnp.float32)
    for iteration in range(ITERS):
        partial_coeff = jnp.zeros((measured.shape[1], coeffs), jnp.float32)
        if iteration == 0:
            partial_coeff = row_scatter(
                vox_parts[0], first_x[:, :half].reshape(-1),
                first.reshape(-1, coeffs), partial_coeff, half, pad,
            )
            partial_coeff = row_scatter(
                vox_parts[1], first_x[:, half:].reshape(-1),
                second.reshape(-1, coeffs), partial_coeff,
            )
        else:
            picked = pick(current, high, low).reshape(blocks, slots)
            local_x = lax.all_to_all(picked, "space", split_axis=0, concat_axis=0, tiled=True)
            local_x = jnp.where(live_here, local_x, 0.0)
            partial_coeff = row_scatter(
                voxel_index, local_x.reshape(-1), local_feat, partial_coeff
            )
        coeff_sum = lax.psum(partial_coeff, "shell")
        if iteration == ITERS - 1:
            residual = (
                jnp.einsum("jg,vj->gv", dictionary, coeff_sum, precision=HI) - measured
            )
        adjoint = jnp.dot(coeff_sum, gram, precision=HI) - data_proj
        local_grad = row_gather_dot(voxel_index, adjoint, local_feat).reshape(blocks, slots)
        local_grad = jnp.where(live_here, local_grad, 0.0)
        grad_slot = lax.all_to_all(local_grad, "space", split_axis=0, concat_axis=0, tiled=True)
        gradient = spread(grad_slot, high, low)
        current = jnp.maximum(current - scaling * gradient, 0.0)
    return (current, residual)


def solution(mesh):
    in_specs = (
        P(("space", "shell")),
        P("space", "shell", None, None),
        P("space", "shell", None, None, None),
        P("space", "shell", None),
        P("space", "shell", None, None),
        P(None, "shell"),
        P("shell", "space"),
    )
    out_specs = (P(("space", "shell")), P("shell", "space"))
    return jax.shard_map(
        on_device, mesh=mesh, in_specs=in_specs, out_specs=out_specs, check_vma=False
    )
```
